256 devices in a mesh: grp: 4 (over x), ctx: 64 (over y, z, core).
Axes of the slice: x: 4, y: 4, z: 8, core: 2. Of those that a mesh axis runs over, the one named last changes fastest.
Arguments:
- queries: bfloat16 [32768, 1792], P(('grp', 'ctx')), may hold values from -100 to 100
- keys: bfloat16 [32768, 1792], P(('grp', 'ctx')), may hold values from -5 to 5
- values: bfloat16 [32768, 1792], P(('grp', 'ctx')), may hold values from -6 to 6
- grad_out: bfloat16 [32768, 1792], P(('grp', 'ctx')), may hold values from -6 to 6
- offsets: int32 [256], replicated, may hold values from 0 to 32768, as said below
Outputs:
- grad_queries: bfloat16 [32768, 1792], P(('grp', 'ctx'))
- grad_keys: bfloat16 [32768, 1792], P(('grp', 'ctx'))
- grad_values: bfloat16 [32768, 1792], P(('grp', 'ctx'))
The draws below stay inside these ranges and needn't reach their ends.
Inputs may be any that keep to these rules, and one draw needn't show every extreme that they name: offsets[0] = 0 and the entries never fall; between consecutive entries below 32768 the difference is 128 to 384, one difference equals 384 exactly; after the last document that starts below 32768 every entry equals 32768, and that document ends at the slab's end.
All inputs are finite; a program needn't handle non-finite values.
Results may differ from the reference program's by a relative error of at most 0.0055.
Values may be sent and summed in bfloat16 or wider, within the bound.
No kernel may reach another device: no remote copies, remote signals or barrier semaphores. Data moves between devices by JAX's collectives and lax.ppermute only.
A program may use at most 64 MiB of HBM per device.

```python
import jax
import jax.numpy as jnp
from jax import lax

HEADS = 14
HEAD_DIM = 128
TOK_DEV = 128
DOC_MAX = 384
FEATURES = 1792
MAXP = 3
TOKENS = 32768
NDOCS = 256


def key_field(key):
    base = jax.random.normal(jax.random.fold_in(key, 71), (TOKENS, HEADS * HEAD_DIM), jnp.float32)
    return jnp.clip(base, -5.0, 5.0)


def draw_keys(key, part):
    field = key_field(key)
    return field.astype(jnp.bfloat16)


def draw_queries(key, part):
    noise = jax.random.normal(jax.random.fold_in(key, 83), (TOKENS, HEADS * HEAD_DIM), jnp.float32)
    noise = jnp.clip(noise, -5.0, 5.0)
    return noise.astype(jnp.bfloat16)


def draw_offsets(key, part):
    lengths = jax.random.randint(jax.random.fold_in(key, 5), (NDOCS,), TOK_DEV, DOC_MAX + 1, dtype=jnp.int32)
    chosen = jax.random.randint(jax.random.fold_in(key, 6), (), 0, min(8, NDOCS), dtype=jnp.int32)
    lengths = jnp.where(jnp.arange(NDOCS, dtype=jnp.int32) == chosen, DOC_MAX, lengths)
    starts = jnp.cumsum(lengths) - lengths
    return jnp.minimum(starts, TOKENS).astype(jnp.int32)


def level_of(stream_key, shape, shards, low, top_value):
    def one(dim, shards_of):
        steps = jax.random.uniform(jax.random.fold_in(jax.random.fold_in(stream_key, 6), dim), (shards_of,), jnp.float32, low / len(shards), top_value / len(shards))
        return jnp.repeat(jnp.exp(steps), shape[dim] // shards_of).reshape((-1,) + (1,) * (len(shape) - dim - 1))

    level = one(*shards[0])
    for cut in shards[1:]:
        level = level * one(*cut)
    return level


def centred(rng, dims, deviation, most, shards=(), kind=jnp.bfloat16):
    gain = level_of(rng, dims, shards, -0.22, 0.18) if shards else 1.0
    entries = jax.random.normal(rng, dims, jnp.float32) * deviation * gain
    return jnp.minimum(jnp.maximum(entries, -most), most).astype(kind)


def setup_inputs(seed: int = 0) -> dict:
    streams_of = jax.random.split(jax.random.key(seed), 6)
    queries = draw_queries(jax.random.fold_in(streams_of[5], 71), 0)
    keys = draw_keys(jax.random.fold_in(streams_of[5], 71), 0)
    values = centred(streams_of[2], (TOKENS, FEATURES), 1.0, 6.0, ((0, 256),))
    grad_out = centred(streams_of[3], (TOKENS, FEATURES), 1.0, 6.0, ((0, 256),))
    offsets = draw_offsets(jax.random.fold_in(streams_of[5], 71), 0)
    return dict(queries=queries, keys=keys, values=values, grad_out=grad_out, offsets=offsets)


NEG = -1.0e30


def segments(offsets, positions, slab_len):
    found = jnp.sum((offsets[None, :] <= positions[:, None]).astype(jnp.int32), axis=1) - 1
    inside = (positions >= 0) & (positions < slab_len)
    return jnp.where(inside, found, -1)


def split_heads(block):
    return block.astype(jnp.float32).reshape(block.shape[0], HEADS, HEAD_DIM)


def rounded(block):
    return lax.optimization_barrier(block.astype(jnp.bfloat16)).astype(jnp.float32)


def pair_statistics(query_rows, grad_rows, row_segments, key_cols, value_cols, col_segments):
    allowed = (row_segments[:, None] == col_segments[None, :])[None]
    scores = jnp.einsum("qhd,khd->hqk", split_heads(query_rows), split_heads(key_cols)) * HEAD_DIM ** -0.5
    scores = jnp.where(allowed, scores, NEG)
    maximum = jnp.max(scores, axis=2)
    probs = jnp.where(allowed, jnp.exp(scores - maximum[:, :, None]), 0.0)
    dprobs = jnp.einsum("qhd,khd->hqk", split_heads(grad_rows), split_heads(value_cols))
    return maximum, jnp.sum(probs, axis=2), jnp.sum(probs * dprobs, axis=2)


def merge_statistics(first, second):
    maximum = jnp.maximum(first[0], second[0])
    scale_one = jnp.exp(first[0] - maximum)
    scale_two = jnp.exp(second[0] - maximum)
    return maximum, first[1] * scale_one + second[1] * scale_two, first[2] * scale_one + second[2] * scale_two


def finalize(statistics):
    return statistics[0] + jnp.log(statistics[1]), statistics[2] / statistics[1]


def pair_gradients(query_rows, grad_rows, row_segments, log_total, delta_rows, key_cols, value_cols, col_segments):
    allowed = (row_segments[:, None] == col_segments[None, :])[None]
    scale = HEAD_DIM ** -0.5
    scores = jnp.einsum("qhd,khd->hqk", split_heads(query_rows), split_heads(key_cols)) * scale
    probs = jnp.where(allowed, jnp.exp(scores - log_total[:, :, None]), 0.0)
    dprobs = jnp.einsum("qhd,khd->hqk", split_heads(grad_rows), split_heads(value_cols))
    dscores = jnp.where(allowed, probs * (dprobs - delta_rows[:, :, None]), 0.0)
    probs_low = rounded(probs)
    dscores_low = rounded(dscores)
    length = query_rows.shape[0]
    grad_query = jnp.einsum("hqk,khd->qhd", dscores_low, split_heads(key_cols)) * scale
    grad_key = jnp.einsum("hqk,qhd->khd", dscores_low, split_heads(query_rows)) * scale
    grad_value = jnp.einsum("hqk,qhd->khd", probs_low, split_heads(grad_rows))
    return (grad_query.reshape(length, FEATURES), grad_key.reshape(length, FEATURES), grad_value.reshape(length, FEATURES))


def reference(queries, keys, values, grad_out, offsets):
    blocks = TOKENS // TOK_DEV
    margin = MAXP * TOK_DEV
    padded_q = jnp.pad(queries, ((margin, margin), (0, 0)))
    padded_k = jnp.pad(keys, ((margin, margin), (0, 0)))
    padded_v = jnp.pad(values, ((margin, margin), (0, 0)))
    padded_o = jnp.pad(grad_out, ((margin, margin), (0, 0)))
    positions = jnp.arange(-margin, TOKENS + margin, dtype=jnp.int32)
    seg_all = segments(offsets, positions, TOKENS)

    def take(array, first):
        return lax.dynamic_slice_in_dim(array, first, TOK_DEV, 0)

    def block_statistics(block):
        base = (block + MAXP) * TOK_DEV
        query_rows = take(padded_q, base)
        grad_rows = take(padded_o, base)
        row_segments = take(seg_all, base)
        result = pair_statistics(query_rows, grad_rows, row_segments, take(padded_k, base), take(padded_v, base), row_segments)
        for distance in range(-MAXP, MAXP + 1):
            if distance != 0:
                other = base + distance * TOK_DEV
                result = merge_statistics(result, pair_statistics(query_rows, grad_rows, row_segments, take(padded_k, other), take(padded_v, other), take(seg_all, other)))
        return finalize(result)

    log_total, delta_rows = lax.map(block_statistics, jnp.arange(blocks, dtype=jnp.int32))
    padded_total = jnp.pad(log_total, ((MAXP, MAXP), (0, 0), (0, 0)))
    padded_delta = jnp.pad(delta_rows, ((MAXP, MAXP), (0, 0), (0, 0)))

    def block_gradients(block):
        base = (block + MAXP) * TOK_DEV
        query_rows = take(padded_q, base)
        grad_rows = take(padded_o, base)
        key_cols = take(padded_k, base)
        value_cols = take(padded_v, base)
        row_segments = take(seg_all, base)
        own_total = padded_total[block + MAXP]
        own_delta = padded_delta[block + MAXP]
        grad_query, grad_key, grad_value = pair_gradients(query_rows, grad_rows, row_segments, own_total, own_delta, key_cols, value_cols, row_segments)
        for distance in range(-MAXP, MAXP + 1):
            if distance != 0:
                other = base + distance * TOK_DEV
                other_block = block + MAXP + distance
                other_segments = take(seg_all, other)
                forward_terms = pair_gradients(query_rows, grad_rows, row_segments, own_total, own_delta, take(padded_k, other), take(padded_v, other), other_segments)
                grad_query = grad_query + rounded(forward_terms[0])
                reverse_terms = pair_gradients(take(padded_q, other), take(padded_o, other), other_segments, padded_total[other_block], padded_delta[other_block], key_cols, value_cols, row_segments)
                grad_key = grad_key + rounded(reverse_terms[1])
                grad_value = grad_value + rounded(reverse_terms[2])
        return (grad_query.astype(jnp.bfloat16), grad_key.astype(jnp.bfloat16), grad_value.astype(jnp.bfloat16))

    grad_queries, grad_keys, grad_values = lax.map(block_gradients, jnp.arange(blocks, dtype=jnp.int32))
    return (grad_queries.reshape(TOKENS, FEATURES), grad_keys.reshape(TOKENS, FEATURES), grad_values.reshape(TOKENS, FEATURES))
```

```python
import jax
import jax.numpy as jnp
from jax import lax
from jax.sharding import PartitionSpec as P

HEADS = 14
HEAD_DIM = 128
MAXP = 3


NEG = -1e30


def shifted(value, axis, by):
    peers = lax.axis_size(axis)
    pairs = [(i, i + by) for i in range(peers) if 0 <= i + by < peers]
    return lax.ppermute(value, axis, pairs)


def segments(offsets, positions, slab_len):
    found = jnp.sum((offsets[None, :] <= positions[:, None]).astype(jnp.int32), axis=1) - 1
    inside = (positions >= 0) & (positions < slab_len)
    return jnp.where(inside, found, -1)


def heads_major(block):
    return block.reshape(block.shape[0], HEADS, HEAD_DIM).transpose(1, 0, 2)


def tokens_major(block):
    return block.transpose(1, 0, 2).reshape(block.shape[1], HEADS * HEAD_DIM)


def rounded(block):
    return lax.optimization_barrier(block.astype(jnp.bfloat16)).astype(jnp.float32)


def pair_statistics(query_rows, grad_rows, row_segments, key_cols, value_cols, col_segments):
    allowed = (row_segments[:, None] == col_segments[None, :])[None]
    scores = jnp.einsum(
        "hqd,hkd->hqk", query_rows, key_cols, preferred_element_type=jnp.float32
    ) * HEAD_DIM ** (-0.5)
    scores = jnp.where(allowed, scores, NEG)
    maximum = jnp.max(scores, axis=2)
    probs = jnp.where(allowed, jnp.exp(scores - maximum[:, :, None]), 0.0)
    dprobs = jnp.einsum(
        "hqd,hkd->hqk", grad_rows, value_cols, preferred_element_type=jnp.float32
    )
    return (maximum, jnp.sum(probs, axis=2), jnp.sum(probs * dprobs, axis=2))


def merge_statistics(first, second):
    maximum = jnp.maximum(first[0], second[0])
    scale_one = jnp.exp(first[0] - maximum)
    scale_two = jnp.exp(second[0] - maximum)
    return (
        maximum,
        first[1] * scale_one + second[1] * scale_two,
        first[2] * scale_one + second[2] * scale_two,
    )


def finalize(statistics):
    return (statistics[0] + jnp.log(statistics[1]), statistics[2] / statistics[1])


def pair_gradients(
    query_rows, grad_rows, row_segments, log_total, delta_rows, key_cols, value_cols, col_segments
):
    allowed = (row_segments[:, None] == col_segments[None, :])[None]
    scale = HEAD_DIM ** (-0.5)
    scores = (
        jnp.einsum("hqd,hkd->hqk", query_rows, key_cols, preferred_element_type=jnp.float32)
        * scale
    )
    probs = jnp.where(allowed, jnp.exp(scores - log_total[:, :, None]), 0.0)
    dprobs = jnp.einsum("hqd,hkd->hqk", grad_rows, value_cols, preferred_element_type=jnp.float32)
    dscores = jnp.where(allowed, probs * (dprobs - delta_rows[:, :, None]), 0.0)
    probs_low = probs.astype(jnp.bfloat16)
    dscores_low = dscores.astype(jnp.bfloat16)
    grad_query = (
        jnp.einsum("hqk,hkd->hqd", dscores_low, key_cols, preferred_element_type=jnp.float32)
        * scale
    )
    grad_key = (
        jnp.einsum("hqk,hqd->hkd", dscores_low, query_rows, preferred_element_type=jnp.float32)
        * scale
    )
    grad_value = jnp.einsum(
        "hqk,hqd->hkd", probs_low, grad_rows, preferred_element_type=jnp.float32
    )
    return grad_query, grad_key, grad_value


def on_device(queries, keys, values, grad_out, offsets):
    axis = ("grp", "ctx")
    block_len = queries.shape[0]
    device_count = lax.axis_size(axis)
    slab_len = device_count * block_len
    device_index = lax.axis_index(axis)
    own_positions = device_index * block_len + jnp.arange(block_len, dtype=jnp.int32)
    own_segments = segments(offsets, own_positions, slab_len)
    query_h = heads_major(queries)
    grad_h = heads_major(grad_out)
    key_h = heads_major(keys)
    value_h = heads_major(values)
    distances = [d for d in range(1, MAXP + 1)] + [-d for d in range(1, MAXP + 1)]

    received = {}
    for distance in distances:
        far_query, far_grad = shifted((query_h, grad_h), axis, -distance)
        far_segments = segments(offsets, own_positions + distance * block_len, slab_len)
        received[distance] = (far_query, far_grad, far_segments)

    row_stats = pair_statistics(query_h, grad_h, own_segments, key_h, value_h, own_segments)
    for distance in distances:
        far_query, far_grad, far_segments = received[distance]
        partial = pair_statistics(far_query, far_grad, far_segments, key_h, value_h, own_segments)
        returned = shifted(partial, axis, distance)
        row_stats = merge_statistics(row_stats, returned)
    log_total, delta_rows = finalize(row_stats)

    grad_query, grad_key, grad_value = pair_gradients(
        query_h, grad_h, own_segments, log_total, delta_rows, key_h, value_h, own_segments
    )
    for distance in distances:
        far_query, far_grad, far_segments = received[distance]
        far_total, far_delta = shifted((log_total, delta_rows), axis, -distance)
        far_gq, far_gk, far_gv = pair_gradients(
            far_query, far_grad, far_segments, far_total, far_delta, key_h, value_h, own_segments
        )
        grad_key = grad_key + rounded(far_gk)
        grad_value = grad_value + rounded(far_gv)
        back_query = shifted(far_gq.astype(jnp.bfloat16), axis, distance)
        grad_query = grad_query + back_query.astype(jnp.float32)
    return (
        tokens_major(grad_query.astype(jnp.bfloat16)),
        tokens_major(grad_key.astype(jnp.bfloat16)),
        tokens_major(grad_value.astype(jnp.bfloat16)),
    )


def solution(mesh):
    placed = (
        P(("grp", "ctx"), None),
        P(("grp", "ctx"), None),
        P(("grp", "ctx"), None),
        P(("grp", "ctx"), None),
        P(),
    )
    return jax.shard_map(
        on_device,
        mesh=mesh,
        in_specs=placed,
        out_specs=(P(("grp", "ctx"), None), P(("grp", "ctx"), None), P(("grp", "ctx"), None)),
        check_vma=False,
    )
```

```python
import jax
import jax.numpy as jnp
from jax import lax
from jax.sharding import PartitionSpec as P

HEADS = 14
HEAD_DIM = 128
MAXP = 3


NEG = -1e30


def shifted(value, axis, by):
    peers = lax.axis_size(axis)
    pairs = [(i, i + by) for i in range(peers) if 0 <= i + by < peers]
    return lax.ppermute(value, axis, pairs)


def segments(offsets, positions, slab_len):
    found = jnp.sum((offsets[None, :] <= positions[:, None]).astype(jnp.int32), axis=1) - 1
    inside = (positions >= 0) & (positions < slab_len)
    return jnp.where(inside, found, -1)


def heads_major(block):
    return block.reshape(block.shape[0], HEADS, HEAD_DIM).transpose(1, 0, 2)


def tokens_major(block):
    return block.transpose(1, 0, 2).reshape(block.shape[1], HEADS * HEAD_DIM)


def rounded(block):
    return lax.optimization_barrier(block.astype(jnp.bfloat16)).astype(jnp.float32)


def pair_statistics(query_rows, grad_rows, row_segments, key_cols, value_cols, col_segments):
    allowed = (row_segments[:, None] == col_segments[None, :])[None]
    scores = jnp.einsum(
        "hqd,hkd->hqk", query_rows, key_cols, preferred_element_type=jnp.float32
    ) * HEAD_DIM ** (-0.5)
    scores = jnp.where(allowed, scores, NEG)
    maximum = jnp.max(scores, axis=2)
    probs = jnp.where(allowed, jnp.exp(scores - maximum[:, :, None]), 0.0)
    dprobs = jnp.einsum(
        "hqd,hkd->hqk", grad_rows, value_cols, preferred_element_type=jnp.float32
    )
    return (maximum, jnp.sum(probs, axis=2), jnp.sum(probs * dprobs, axis=2))


def merge_statistics(first, second):
    maximum = jnp.maximum(first[0], second[0])
    scale_one = jnp.exp(first[0] - maximum)
    scale_two = jnp.exp(second[0] - maximum)
    return (
        maximum,
        first[1] * scale_one + second[1] * scale_two,
        first[2] * scale_one + second[2] * scale_two,
    )


def finalize(statistics):
    return (statistics[0] + jnp.log(statistics[1]), statistics[2] / statistics[1])


def pair_gradients(
    query_rows, grad_rows, row_segments, log_total, delta_rows, key_cols, value_cols, col_segments
):
    allowed = (row_segments[:, None] == col_segments[None, :])[None]
    scale = HEAD_DIM ** (-0.5)
    scores = (
        jnp.einsum("hqd,hkd->hqk", query_rows, key_cols, preferred_element_type=jnp.float32)
        * scale
    )
    probs = jnp.where(allowed, jnp.exp(scores - log_total[:, :, None]), 0.0)
    dprobs = jnp.einsum("hqd,hkd->hqk", grad_rows, value_cols, preferred_element_type=jnp.float32)
    dscores = jnp.where(allowed, probs * (dprobs - delta_rows[:, :, None]), 0.0)
    probs_low = probs.astype(jnp.bfloat16)
    dscores_low = dscores.astype(jnp.bfloat16)
    grad_query = (
        jnp.einsum("hqk,hkd->hqd", dscores_low, key_cols, preferred_element_type=jnp.float32)
        * scale
    )
    grad_key = (
        jnp.einsum("hqk,hqd->hkd", dscores_low, query_rows, preferred_element_type=jnp.float32)
        * scale
    )
    grad_value = jnp.einsum(
        "hqk,hqd->hkd", probs_low, grad_rows, preferred_element_type=jnp.float32
    )
    return grad_query, grad_key, grad_value


def on_device(queries, keys, values, grad_out, offsets):
    axis = ("grp", "ctx")
    block_len = queries.shape[0]
    device_count = lax.axis_size(axis)
    slab_len = device_count * block_len
    device_index = lax.axis_index(axis)
    own_positions = device_index * block_len + jnp.arange(block_len, dtype=jnp.int32)
    own_segments = segments(offsets, own_positions, slab_len)
    query_h = heads_major(queries)
    grad_h = heads_major(grad_out)
    key_h = heads_major(keys)
    value_h = heads_major(values)
    rows_h = jnp.stack([query_h, grad_h])
    distances = [d for d in range(1, MAXP + 1)] + [-d for d in range(1, MAXP + 1)]

    received = {}
    for distance in distances:
        far_rows = shifted(rows_h, axis, -distance)
        far_query, far_grad = far_rows[0], far_rows[1]
        far_segments = segments(offsets, own_positions + distance * block_len, slab_len)
        received[distance] = (far_query, far_grad, far_segments)

    row_stats = pair_statistics(query_h, grad_h, own_segments, key_h, value_h, own_segments)
    for distance in distances:
        far_query, far_grad, far_segments = received[distance]
        partial = pair_statistics(far_query, far_grad, far_segments, key_h, value_h, own_segments)
        returned = shifted(jnp.stack(partial), axis, distance)
        row_stats = merge_statistics(row_stats, (returned[0], returned[1], returned[2]))
    log_total, delta_rows = finalize(row_stats)
    final_stats = jnp.stack([log_total, delta_rows])

    grad_query, grad_key, grad_value = pair_gradients(
        query_h, grad_h, own_segments, log_total, delta_rows, key_h, value_h, own_segments
    )
    for distance in distances:
        far_query, far_grad, far_segments = received[distance]
        far_final = shifted(final_stats, axis, -distance)
        far_total, far_delta = far_final[0], far_final[1]
        far_gq, far_gk, far_gv = pair_gradients(
            far_query, far_grad, far_segments, far_total, far_delta, key_h, value_h, own_segments
        )
        grad_key = grad_key + rounded(far_gk)
        grad_value = grad_value + rounded(far_gv)
        back_query = shifted(far_gq.astype(jnp.bfloat16), axis, distance)
        grad_query = grad_query + back_query.astype(jnp.float32)
    return (
        tokens_major(grad_query.astype(jnp.bfloat16)),
        tokens_major(grad_key.astype(jnp.bfloat16)),
        tokens_major(grad_value.astype(jnp.bfloat16)),
    )


def solution(mesh):
    placed = (
        P(("grp", "ctx"), None),
        P(("grp", "ctx"), None),
        P(("grp", "ctx"), None),
        P(("grp", "ctx"), None),
        P(),
    )
    return jax.shard_map(
        on_device,
        mesh=mesh,
        in_specs=placed,
        out_specs=(P(("grp", "ctx"), None), P(("grp", "ctx"), None), P(("grp", "ctx"), None)),
        check_vma=False,
    )
```

```python
import functools

import jax
import jax.numpy as jnp
from jax import lax
from jax.experimental import pallas as pl
from jax.sharding import PartitionSpec as P

HEADS = 14
HEAD_DIM = 128
MAXP = 3


NEG = -1e30


NT = (((1,), (1,)), ((), ()))
TN = (((0,), (0,)), ((), ()))


def shifted(value, axis, by):
    peers = lax.axis_size(axis)
    pairs = [(i, i + by) for i in range(peers) if 0 <= i + by < peers]
    return lax.ppermute(value, axis, pairs)


def segments(offsets, positions, slab_len):
    found = jnp.sum((offsets[None, :] <= positions[:, None]).astype(jnp.int32), axis=1) - 1
    inside = (positions >= 0) & (positions < slab_len)
    return jnp.where(inside, found, -1)


def stats_kernel(rows_ref, key_ref, value_ref, row_seg_ref, col_seg_ref, out_ref):
    allowed = col_seg_ref[...] == row_seg_ref[...]
    scale = HEAD_DIM ** (-0.5)
    for h in range(HEADS):
        cols = slice(h * HEAD_DIM, (h + 1) * HEAD_DIM)
        query = rows_ref[0, :, cols]
        grad = rows_ref[1, :, cols]
        scores = lax.dot_general(
            key_ref[:, cols], query, NT, preferred_element_type=jnp.float32
        ) * scale
        scores = jnp.where(allowed, scores, NEG)
        maximum = jnp.max(scores, axis=0, keepdims=True)
        probs = jnp.where(allowed, jnp.exp(scores - maximum), 0.0)
        dprobs = lax.dot_general(
            value_ref[:, cols], grad, NT, preferred_element_type=jnp.float32
        )
        out_ref[0, h : h + 1, :] = maximum
        out_ref[1, h : h + 1, :] = jnp.sum(probs, axis=0, keepdims=True)
        out_ref[2, h : h + 1, :] = jnp.sum(probs * dprobs, axis=0, keepdims=True)


def grad_kernel(
    rows_ref, final_ref, key_ref, value_ref, row_seg_ref, col_seg_ref, gq_ref, gk_ref, gv_ref
):
    allowed = col_seg_ref[...] == row_seg_ref[...]
    scale = HEAD_DIM ** (-0.5)
    for h in range(HEADS):
        cols = slice(h * HEAD_DIM, (h + 1) * HEAD_DIM)
        query = rows_ref[0, :, cols]
        grad = rows_ref[1, :, cols]
        key = key_ref[:, cols]
        log_total = final_ref[0, h : h + 1, :]
        delta = final_ref[1, h : h + 1, :]
        scores = lax.dot_general(key, query, NT, preferred_element_type=jnp.float32) * scale
        probs = jnp.where(allowed, jnp.exp(scores - log_total), 0.0)
        dprobs = lax.dot_general(
            value_ref[:, cols], grad, NT, preferred_element_type=jnp.float32
        )
        dscores = jnp.where(allowed, probs * (dprobs - delta), 0.0)
        probs_low = probs.astype(jnp.bfloat16)
        dscores_low = dscores.astype(jnp.bfloat16)
        gk = jnp.dot(dscores_low, query, preferred_element_type=jnp.float32) * scale
        gv = jnp.dot(probs_low, grad, preferred_element_type=jnp.float32)
        gq = lax.dot_general(dscores_low, key, TN, preferred_element_type=jnp.float32) * scale
        gq_ref[:, cols] = gq.astype(gq_ref.dtype)
        gk_ref[:, cols] = gk.astype(gk_ref.dtype)
        gv_ref[:, cols] = gv.astype(gv_ref.dtype)


def pair_statistics(rows, keys, values, row_segments, col_segments):
    return pl.pallas_call(
        stats_kernel,
        out_shape=jax.ShapeDtypeStruct((3, HEADS, rows.shape[1]), jnp.float32),
    )(rows, keys, values, row_segments[None, :], col_segments[:, None])


def pair_gradients(rows, final, keys, values, row_segments, col_segments, out_dtype):
    shape = jax.ShapeDtypeStruct(keys.shape, out_dtype)
    return pl.pallas_call(grad_kernel, out_shape=(shape, shape, shape))(
        rows, final, keys, values, row_segments[None, :], col_segments[:, None]
    )


def merge_statistics(first, second):
    maximum = jnp.maximum(first[0], second[0])
    scale_one = jnp.exp(first[0] - maximum)
    scale_two = jnp.exp(second[0] - maximum)
    return (
        maximum,
        first[1] * scale_one + second[1] * scale_two,
        first[2] * scale_one + second[2] * scale_two,
    )


def finalize(statistics):
    return (statistics[0] + jnp.log(statistics[1]), statistics[2] / statistics[1])


def on_device(queries, keys, values, grad_out, offsets):
    axis = ("grp", "ctx")
    block_len = queries.shape[0]
    device_count = lax.axis_size(axis)
    slab_len = device_count * block_len
    device_index = lax.axis_index(axis)
    own_positions = device_index * block_len + jnp.arange(block_len, dtype=jnp.int32)
    own_segments = segments(offsets, own_positions, slab_len)
    rows = jnp.stack([queries, grad_out])
    distances = [d for d in range(1, MAXP + 1)] + [-d for d in range(1, MAXP + 1)]

    received = {}
    for distance in distances:
        far_rows = shifted(rows, axis, -distance)
        far_segments = segments(offsets, own_positions + distance * block_len, slab_len)
        received[distance] = (far_rows, far_segments)

    own = pair_statistics(rows, keys, values, own_segments, own_segments)
    row_stats = (own[0], own[1], own[2])
    for distance in distances:
        far_rows, far_segments = received[distance]
        partial = pair_statistics(far_rows, keys, values, far_segments, own_segments)
        returned = shifted(partial, axis, distance)
        row_stats = merge_statistics(row_stats, (returned[0], returned[1], returned[2]))
    log_total, delta_rows = finalize(row_stats)
    final_stats = jnp.stack([log_total, delta_rows])

    grad_query, grad_key, grad_value = pair_gradients(
        rows, final_stats, keys, values, own_segments, own_segments, jnp.float32
    )
    for distance in distances:
        far_rows, far_segments = received[distance]
        far_final = shifted(final_stats, axis, -distance)
        far_gq, far_gk, far_gv = pair_gradients(
            far_rows, far_final, keys, values, far_segments, own_segments, jnp.bfloat16
        )
        grad_key = grad_key + far_gk.astype(jnp.float32)
        grad_value = grad_value + far_gv.astype(jnp.float32)
        back_query = shifted(far_gq, axis, distance)
        grad_query = grad_query + back_query.astype(jnp.float32)
    return (
        grad_query.astype(jnp.bfloat16),
        grad_key.astype(jnp.bfloat16),
        grad_value.astype(jnp.bfloat16),
    )


def solution(mesh):
    placed = (
        P(("grp", "ctx"), None),
        P(("grp", "ctx"), None),
        P(("grp", "ctx"), None),
        P(("grp", "ctx"), None),
        P(),
    )
    return jax.shard_map(
        on_device,
        mesh=mesh,
        in_specs=placed,
        out_specs=(P(("grp", "ctx"), None), P(("grp", "ctx"), None), P(("grp", "ctx"), None)),
        check_vma=False,
    )
```

```python
import functools

import jax
import jax.numpy as jnp
from jax import lax
from jax.experimental import pallas as pl
from jax.sharding import PartitionSpec as P

HEADS = 14
HEAD_DIM = 128
MAXP = 3


NEG = -1e30


NT = (((1,), (1,)), ((), ()))
TN = (((0,), (0,)), ((), ()))


def shifted(value, axis, by):
    peers = lax.axis_size(axis)
    pairs = [(i, i + by) for i in range(peers) if 0 <= i + by < peers]
    return lax.ppermute(value, axis, pairs)


def segments(offsets, positions, slab_len):
    found = jnp.sum((offsets[None, :] <= positions[:, None]).astype(jnp.int32), axis=1) - 1
    inside = (positions >= 0) & (positions < slab_len)
    return jnp.where(inside, found, -1)


def stats_kernel(rows_ref, key_ref, value_ref, row_seg_ref, col_seg_ref, out_ref):
    allowed = col_seg_ref[...] == row_seg_ref[...]
    scale = HEAD_DIM ** (-0.5)
    for h in range(HEADS):
        cols = slice(h * HEAD_DIM, (h + 1) * HEAD_DIM)
        query = rows_ref[0, :, cols]
        grad = rows_ref[1, :, cols]
        scores = lax.dot_general(
            key_ref[:, cols], query, NT, preferred_element_type=jnp.float32
        ) * scale
        scores = jnp.where(allowed, scores, NEG)
        maximum = jnp.max(scores, axis=0, keepdims=True)
        probs = jnp.where(allowed, jnp.exp(scores - maximum), 0.0)
        dprobs = lax.dot_general(
            value_ref[:, cols], grad, NT, preferred_element_type=jnp.float32
        )
        out_ref[0, h : h + 1, :] = maximum
        out_ref[1, h : h + 1, :] = jnp.sum(probs, axis=0, keepdims=True)
        out_ref[2, h : h + 1, :] = jnp.sum(probs * dprobs, axis=0, keepdims=True)


def grad_kernel(
    rows_ref, final_ref, key_ref, value_ref, row_seg_ref, col_seg_ref, gq_ref, gk_ref, gv_ref
):
    allowed = col_seg_ref[...] == row_seg_ref[...]
    scale = HEAD_DIM ** (-0.5)
    for h in range(HEADS):
        cols = slice(h * HEAD_DIM, (h + 1) * HEAD_DIM)
        query = rows_ref[0, :, cols]
        grad = rows_ref[1, :, cols]
        key = key_ref[:, cols]
        log_total = final_ref[0, h : h + 1, :]
        delta = final_ref[1, h : h + 1, :]
        scores = lax.dot_general(key, query, NT, preferred_element_type=jnp.float32) * scale
        probs = jnp.where(allowed, jnp.exp(scores - log_total), 0.0)
        dprobs = lax.dot_general(
            value_ref[:, cols], grad, NT, preferred_element_type=jnp.float32
        )
        dscores = jnp.where(allowed, probs * (dprobs - delta), 0.0)
        probs_low = probs.astype(jnp.bfloat16)
        dscores_low = dscores.astype(jnp.bfloat16)
        gk = jnp.dot(dscores_low, query, preferred_element_type=jnp.float32) * scale
        gv = jnp.dot(probs_low, grad, preferred_element_type=jnp.float32)
        gq = lax.dot_general(dscores_low, key, TN, preferred_element_type=jnp.float32) * scale
        gq_ref[:, cols] = gq.astype(gq_ref.dtype)
        gk_ref[:, cols] = gk.astype(gk_ref.dtype)
        gv_ref[:, cols] = gv.astype(gv_ref.dtype)


def pair_statistics(rows, keys, values, row_segments, col_segments):
    return pl.pallas_call(
        stats_kernel,
        out_shape=jax.ShapeDtypeStruct((3, HEADS, rows.shape[1]), jnp.float32),
    )(rows, keys, values, row_segments[None, :], col_segments[:, None])


def pair_gradients(rows, final, keys, values, row_segments, col_segments, out_dtype):
    shape = jax.ShapeDtypeStruct(keys.shape, out_dtype)
    return pl.pallas_call(grad_kernel, out_shape=(shape, shape, shape))(
        rows, final, keys, values, row_segments[None, :], col_segments[:, None]
    )


def merge_statistics(first, second):
    maximum = jnp.maximum(first[0], second[0])
    scale_one = jnp.exp(first[0] - maximum)
    scale_two = jnp.exp(second[0] - maximum)
    return (
        maximum,
        first[1] * scale_one + second[1] * scale_two,
        first[2] * scale_one + second[2] * scale_two,
    )


def finalize(statistics):
    return (statistics[0] + jnp.log(statistics[1]), statistics[2] / statistics[1])


def on_device(queries, keys, values, grad_out, offsets):
    axis = ("grp", "ctx")
    block_len = queries.shape[0]
    device_count = lax.axis_size(axis)
    slab_len = device_count * block_len
    device_index = lax.axis_index(axis)
    own_positions = device_index * block_len + jnp.arange(block_len, dtype=jnp.int32)
    own_segments = segments(offsets, own_positions, slab_len)
    rows = jnp.stack([queries, grad_out])
    distances = [d for d in range(1, MAXP + 1)] + [-d for d in range(1, MAXP + 1)]

    received = {}
    for distance in distances:
        far_rows = shifted(rows, axis, -distance)
        far_segments = segments(offsets, own_positions + distance * block_len, slab_len)
        shared = jnp.any(far_segments[:, None] == own_segments[None, :])
        received[distance] = (far_rows, far_segments, shared)

    own = pair_statistics(rows, keys, values, own_segments, own_segments)
    row_stats = (own[0], own[1], own[2])
    for distance in distances:
        far_rows, far_segments, shared = received[distance]
        partial = lax.cond(
            shared,
            lambda: pair_statistics(far_rows, keys, values, far_segments, own_segments),
            lambda: jnp.stack(
                [
                    jnp.full((HEADS, block_len), NEG, jnp.float32),
                    jnp.zeros((HEADS, block_len), jnp.float32),
                    jnp.zeros((HEADS, block_len), jnp.float32),
                ]
            ),
        )
        returned = shifted(partial, axis, distance)
        row_stats = merge_statistics(row_stats, (returned[0], returned[1], returned[2]))
    log_total, delta_rows = finalize(row_stats)
    final_stats = jnp.stack([log_total, delta_rows])

    grad_query, grad_key, grad_value = pair_gradients(
        rows, final_stats, keys, values, own_segments, own_segments, jnp.float32
    )
    for distance in distances:
        far_rows, far_segments, shared = received[distance]
        far_final = shifted(final_stats, axis, -distance)
        far_gq, far_gk, far_gv = lax.cond(
            shared,
            lambda: pair_gradients(
                far_rows, far_final, keys, values, far_segments, own_segments, jnp.bfloat16
            ),
            lambda: (jnp.zeros(keys.shape, jnp.bfloat16),) * 3,
        )
        grad_key = grad_key + far_gk.astype(jnp.float32)
        grad_value = grad_value + far_gv.astype(jnp.float32)
        back_query = shifted(far_gq, axis, distance)
        grad_query = grad_query + back_query.astype(jnp.float32)
    return (
        grad_query.astype(jnp.bfloat16),
        grad_key.astype(jnp.bfloat16),
        grad_value.astype(jnp.bfloat16),
    )


def solution(mesh):
    placed = (
        P(("grp", "ctx"), None),
        P(("grp", "ctx"), None),
        P(("grp", "ctx"), None),
        P(("grp", "ctx"), None),
        P(),
    )
    return jax.shard_map(
        on_device,
        mesh=mesh,
        in_specs=placed,
        out_specs=(P(("grp", "ctx"), None), P(("grp", "ctx"), None), P(("grp", "ctx"), None)),
        check_vma=False,
    )
```

```python
import functools

import jax
import jax.numpy as jnp
from jax import lax
from jax.experimental import pallas as pl
from jax.sharding import PartitionSpec as P

HEADS = 14
HEAD_DIM = 128
MAXP = 3


NEG = -1e30


NT = (((1,), (1,)), ((), ()))
TN = (((0,), (0,)), ((), ()))


def shifted(value, axis, by):
    peers = lax.axis_size(axis)
    pairs = [(i, i + by) for i in range(peers) if 0 <= i + by < peers]
    return lax.ppermute(value, axis, pairs)


def segments(offsets, positions, slab_len):
    found = jnp.sum((offsets[None, :] <= positions[:, None]).astype(jnp.int32), axis=1) - 1
    inside = (positions >= 0) & (positions < slab_len)
    return jnp.where(inside, found, -1)


def stats_kernel(rows_ref, kv_ref, row_seg_ref, col_seg_ref, out_ref):
    allowed = col_seg_ref[...] == row_seg_ref[...]
    scale = HEAD_DIM ** (-0.5)
    for h in range(HEADS):
        cols = slice(h * HEAD_DIM, (h + 1) * HEAD_DIM)
        query = rows_ref[0, :, cols]
        grad = rows_ref[1, :, cols]
        scores = lax.dot_general(
            kv_ref[0, :, cols], query, NT, preferred_element_type=jnp.float32
        ) * scale
        scores = jnp.where(allowed, scores, NEG)
        maximum = jnp.max(scores, axis=0, keepdims=True)
        probs = jnp.where(allowed, jnp.exp(scores - maximum), 0.0)
        dprobs = lax.dot_general(
            kv_ref[1, :, cols], grad, NT, preferred_element_type=jnp.float32
        )
        out_ref[0, h : h + 1, :] = maximum
        out_ref[1, h : h + 1, :] = jnp.sum(probs, axis=0, keepdims=True)
        out_ref[2, h : h + 1, :] = jnp.sum(probs * dprobs, axis=0, keepdims=True)


def grad_kernel(rows_ref, final_ref, kv_ref, row_seg_ref, col_seg_ref, gq_ref, gkv_ref):
    allowed = col_seg_ref[...] == row_seg_ref[...]
    scale = HEAD_DIM ** (-0.5)
    for h in range(HEADS):
        cols = slice(h * HEAD_DIM, (h + 1) * HEAD_DIM)
        query = rows_ref[0, :, cols]
        grad = rows_ref[1, :, cols]
        key = kv_ref[0, :, cols]
        log_total = final_ref[0, h : h + 1, :]
        delta = final_ref[1, h : h + 1, :]
        scores = lax.dot_general(key, query, NT, preferred_element_type=jnp.float32) * scale
        probs = jnp.where(allowed, jnp.exp(scores - log_total), 0.0)
        dprobs = lax.dot_general(
            kv_ref[1, :, cols], grad, NT, preferred_element_type=jnp.float32
        )
        dscores = jnp.where(allowed, probs * (dprobs - delta), 0.0)
        probs_low = probs.astype(jnp.bfloat16)
        dscores_low = dscores.astype(jnp.bfloat16)
        gk = jnp.dot(dscores_low, query, preferred_element_type=jnp.float32) * scale
        gv = jnp.dot(probs_low, grad, preferred_element_type=jnp.float32)
        gq = lax.dot_general(dscores_low, key, TN, preferred_element_type=jnp.float32) * scale
        gq_ref[:, cols] = gq.astype(gq_ref.dtype)
        gkv_ref[0, :, cols] = gk.astype(gkv_ref.dtype)
        gkv_ref[1, :, cols] = gv.astype(gkv_ref.dtype)


def pair_statistics(rows, kv, row_segments, col_segments):
    return pl.pallas_call(
        stats_kernel,
        out_shape=jax.ShapeDtypeStruct((3, HEADS, rows.shape[1]), jnp.float32),
    )(rows, kv, row_segments[None, :], col_segments[:, None])


def pair_gradients(rows, final, kv, row_segments, col_segments, out_dtype):
    return pl.pallas_call(
        grad_kernel,
        out_shape=(
            jax.ShapeDtypeStruct(rows.shape[1:], out_dtype),
            jax.ShapeDtypeStruct(kv.shape, out_dtype),
        ),
    )(rows, final, kv, row_segments[None, :], col_segments[:, None])


def merge_statistics(first, second):
    maximum = jnp.maximum(first[0], second[0])
    scale_one = jnp.exp(first[0] - maximum)
    scale_two = jnp.exp(second[0] - maximum)
    return (
        maximum,
        first[1] * scale_one + second[1] * scale_two,
        first[2] * scale_one + second[2] * scale_two,
    )


def finalize(statistics):
    return (statistics[0] + jnp.log(statistics[1]), statistics[2] / statistics[1])


def on_device(queries, keys, values, grad_out, offsets):
    axis = ("grp", "ctx")
    block_len = queries.shape[0]
    device_count = lax.axis_size(axis)
    slab_len = device_count * block_len
    device_index = lax.axis_index(axis)
    own_positions = device_index * block_len + jnp.arange(block_len, dtype=jnp.int32)
    own_segments = segments(offsets, own_positions, slab_len)
    rows = jnp.stack([queries, grad_out])
    kv = jnp.stack([keys, values])
    distances = [d for d in range(1, MAXP + 1)] + [-d for d in range(1, MAXP + 1)]

    received = {}
    for distance in distances:
        far_kv = shifted(kv, axis, -distance)
        far_segments = segments(offsets, own_positions + distance * block_len, slab_len)
        shared = jnp.any(far_segments[:, None] == own_segments[None, :])
        received[distance] = (far_kv, far_segments, shared)

    own = pair_statistics(rows, kv, own_segments, own_segments)
    row_stats = (own[0], own[1], own[2])
    for distance in distances:
        far_kv, far_segments, shared = received[distance]
        partial = lax.cond(
            shared,
            lambda: pair_statistics(rows, far_kv, own_segments, far_segments),
            lambda: jnp.stack(
                [
                    jnp.full((HEADS, block_len), NEG, jnp.float32),
                    jnp.zeros((HEADS, block_len), jnp.float32),
                    jnp.zeros((HEADS, block_len), jnp.float32),
                ]
            ),
        )
        row_stats = merge_statistics(row_stats, (partial[0], partial[1], partial[2]))
    log_total, delta_rows = finalize(row_stats)
    final_stats = jnp.stack([log_total, delta_rows])

    grad_query, grad_kv = pair_gradients(
        rows, final_stats, kv, own_segments, own_segments, jnp.float32
    )
    for distance in distances:
        far_kv, far_segments, shared = received[distance]
        far_gq, far_gkv = lax.cond(
            shared,
            lambda: pair_gradients(
                rows, final_stats, far_kv, own_segments, far_segments, jnp.bfloat16
            ),
            lambda: (
                jnp.zeros(queries.shape, jnp.bfloat16),
                jnp.zeros(kv.shape, jnp.bfloat16),
            ),
        )
        grad_query = grad_query + far_gq.astype(jnp.float32)
        back_kv = shifted(far_gkv, axis, distance)
        grad_kv = grad_kv + back_kv.astype(jnp.float32)
    return (
        grad_query.astype(jnp.bfloat16),
        grad_kv[0].astype(jnp.bfloat16),
        grad_kv[1].astype(jnp.bfloat16),
    )


def solution(mesh):
    placed = (
        P(("grp", "ctx"), None),
        P(("grp", "ctx"), None),
        P(("grp", "ctx"), None),
        P(("grp", "ctx"), None),
        P(),
    )
    return jax.shard_map(
        on_device,
        mesh=mesh,
        in_specs=placed,
        out_specs=(P(("grp", "ctx"), None), P(("grp", "ctx"), None), P(("grp", "ctx"), None)),
        check_vma=False,
    )
```

```python
import functools

import jax
import jax.numpy as jnp
from jax import lax
from jax.experimental import pallas as pl
from jax.sharding import PartitionSpec as P

HEADS = 14
HEAD_DIM = 128
MAXP = 3


NEG = -1e30


NT = (((1,), (1,)), ((), ()))
TN = (((0,), (0,)), ((), ()))


def shifted(value, axis, by):
    peers = lax.axis_size(axis)
    pairs = [(i, i + by) for i in range(peers) if 0 <= i + by < peers]
    return lax.ppermute(value, axis, pairs)


def segments(offsets, positions, slab_len):
    found = jnp.sum((offsets[None, :] <= positions[:, None]).astype(jnp.int32), axis=1) - 1
    inside = (positions >= 0) & (positions < slab_len)
    return jnp.where(inside, found, -1)


def allowed_of(row_seg_ref, col_seg_ref):
    width = row_seg_ref.shape[1]
    cols = jnp.transpose(jnp.broadcast_to(col_seg_ref[...], (width, width)))
    return cols == row_seg_ref[...]


def stats_kernel(rows_ref, kv_ref, row_seg_ref, col_seg_ref, out_ref):
    allowed = allowed_of(row_seg_ref, col_seg_ref)
    scale = HEAD_DIM ** (-0.5)
    for h in range(HEADS):
        cols = slice(h * HEAD_DIM, (h + 1) * HEAD_DIM)
        query = rows_ref[0, :, cols]
        grad = rows_ref[1, :, cols]
        scores = lax.dot_general(
            kv_ref[0, :, cols], query, NT, preferred_element_type=jnp.float32
        ) * scale
        scores = jnp.where(allowed, scores, NEG)
        maximum = jnp.max(scores, axis=0, keepdims=True)
        probs = jnp.where(allowed, jnp.exp(scores - maximum), 0.0)
        dprobs = lax.dot_general(
            kv_ref[1, :, cols], grad, NT, preferred_element_type=jnp.float32
        )
        out_ref[0, h : h + 1, :] = maximum
        out_ref[1, h : h + 1, :] = jnp.sum(probs, axis=0, keepdims=True)
        out_ref[2, h : h + 1, :] = jnp.sum(probs * dprobs, axis=0, keepdims=True)


def grad_kernel(rows_ref, final_ref, kv_ref, row_seg_ref, col_seg_ref, *refs):
    if len(refs) == 3:
        acc_ref, gq_ref, gkv_ref = refs
    else:
        acc_ref = None
        gq_ref, gkv_ref = refs
    allowed = allowed_of(row_seg_ref, col_seg_ref)
    scale = HEAD_DIM ** (-0.5)
    for h in range(HEADS):
        cols = slice(h * HEAD_DIM, (h + 1) * HEAD_DIM)
        query = rows_ref[0, :, cols]
        grad = rows_ref[1, :, cols]
        key = kv_ref[0, :, cols]
        log_total = final_ref[0, h : h + 1, :]
        delta = final_ref[1, h : h + 1, :]
        scores = lax.dot_general(key, query, NT, preferred_element_type=jnp.float32) * scale
        probs = jnp.where(allowed, jnp.exp(scores - log_total), 0.0)
        dprobs = lax.dot_general(
            kv_ref[1, :, cols], grad, NT, preferred_element_type=jnp.float32
        )
        dscores = jnp.where(allowed, probs * (dprobs - delta), 0.0)
        probs_low = probs.astype(jnp.bfloat16)
        dscores_low = dscores.astype(jnp.bfloat16)
        gk = jnp.dot(dscores_low, query, preferred_element_type=jnp.float32) * scale
        gv = jnp.dot(probs_low, grad, preferred_element_type=jnp.float32)
        gq = lax.dot_general(dscores_low, key, TN, preferred_element_type=jnp.float32) * scale
        if acc_ref is None:
            gq_ref[:, cols] = gq
        else:
            gq_ref[:, cols] = acc_ref[:, cols] + gq.astype(jnp.bfloat16).astype(jnp.float32)
        gkv_ref[0, :, cols] = gk.astype(gkv_ref.dtype)
        gkv_ref[1, :, cols] = gv.astype(gkv_ref.dtype)


def pair_statistics(rows, kv, row_segments, col_segments):
    return pl.pallas_call(
        stats_kernel,
        out_shape=jax.ShapeDtypeStruct((3, HEADS, rows.shape[1]), jnp.float32),
    )(rows, kv, row_segments[None, :], col_segments[None, :])


def pair_gradients(rows, final, kv, row_segments, col_segments, accumulator=None):
    operands = [rows, final, kv, row_segments[None, :], col_segments[None, :]]
    gq_shape = jax.ShapeDtypeStruct(rows.shape[1:], jnp.float32)
    if accumulator is None:
        kv_shape = jax.ShapeDtypeStruct(kv.shape, jnp.float32)
        return pl.pallas_call(grad_kernel, out_shape=(gq_shape, kv_shape))(*operands)
    kv_shape = jax.ShapeDtypeStruct(kv.shape, jnp.bfloat16)
    return pl.pallas_call(
        grad_kernel,
        out_shape=(gq_shape, kv_shape),
        input_output_aliases={len(operands): 0},
    )(*operands, accumulator)


def merge_statistics(first, second):
    maximum = jnp.maximum(first[0], second[0])
    scale_one = jnp.exp(first[0] - maximum)
    scale_two = jnp.exp(second[0] - maximum)
    return (
        maximum,
        first[1] * scale_one + second[1] * scale_two,
        first[2] * scale_one + second[2] * scale_two,
    )


def finalize(statistics):
    return (statistics[0] + jnp.log(statistics[1]), statistics[2] / statistics[1])


def on_device(queries, keys, values, grad_out, offsets):
    axis = ("grp", "ctx")
    block_len = queries.shape[0]
    device_count = lax.axis_size(axis)
    slab_len = device_count * block_len
    device_index = lax.axis_index(axis)
    own_positions = device_index * block_len + jnp.arange(block_len, dtype=jnp.int32)
    own_segments = segments(offsets, own_positions, slab_len)
    rows = jnp.stack([queries, grad_out])
    kv = jnp.stack([keys, values])
    distances = [d for d in range(1, MAXP + 1)] + [-d for d in range(1, MAXP + 1)]

    received = {}
    for distance in distances:
        far_kv = shifted(kv, axis, -distance)
        far_segments = segments(offsets, own_positions + distance * block_len, slab_len)
        shared = jnp.any(far_segments[:, None] == own_segments[None, :])
        received[distance] = (far_kv, far_segments, shared)

    own = pair_statistics(rows, kv, own_segments, own_segments)
    row_stats = (own[0], own[1], own[2])
    for distance in distances:
        far_kv, far_segments, shared = received[distance]

        def merged(row_stats=row_stats, far_kv=far_kv, far_segments=far_segments):
            partial = pair_statistics(rows, far_kv, own_segments, far_segments)
            return merge_statistics(row_stats, (partial[0], partial[1], partial[2]))

        row_stats = lax.cond(shared, merged, lambda: row_stats)
    log_total, delta_rows = finalize(row_stats)
    final_stats = jnp.stack([log_total, delta_rows])

    grad_query, grad_kv = pair_gradients(rows, final_stats, kv, own_segments, own_segments)
    for distance in distances:
        far_kv, far_segments, shared = received[distance]
        grad_query, far_gkv = lax.cond(
            shared,
            lambda: pair_gradients(
                rows, final_stats, far_kv, own_segments, far_segments, grad_query
            ),
            lambda: (grad_query, far_kv),
        )
        back_kv = shifted(far_gkv, axis, distance)
        back_shared = received[-distance][2]
        grad_kv = grad_kv + jnp.where(back_shared, back_kv.astype(jnp.float32), 0.0)
    return (
        grad_query.astype(jnp.bfloat16),
        grad_kv[0].astype(jnp.bfloat16),
        grad_kv[1].astype(jnp.bfloat16),
    )


def solution(mesh):
    placed = (
        P(("grp", "ctx"), None),
        P(("grp", "ctx"), None),
        P(("grp", "ctx"), None),
        P(("grp", "ctx"), None),
        P(),
    )
    return jax.shard_map(
        on_device,
        mesh=mesh,
        in_specs=placed,
        out_specs=(P(("grp", "ctx"), None), P(("grp", "ctx"), None), P(("grp", "ctx"), None)),
        check_vma=False,
    )
```

```python
import functools

import jax
import jax.numpy as jnp
from jax import lax
from jax.experimental import pallas as pl
from jax.experimental.pallas import tpu as pltpu
from jax.sharding import PartitionSpec as P

HEADS = 14
HEAD_DIM = 128
MAXP = 3


NEG = -1e30


NT = (((1,), (1,)), ((), ()))
TN = (((0,), (0,)), ((), ()))


def shifted(value, axis, by):
    peers = lax.axis_size(axis)
    pairs = [(i, i + by) for i in range(peers) if 0 <= i + by < peers]
    return lax.ppermute(value, axis, pairs)


def segments(offsets, positions, slab_len):
    found = jnp.sum((offsets[None, :] <= positions[:, None]).astype(jnp.int32), axis=1) - 1
    inside = (positions >= 0) & (positions < slab_len)
    return jnp.where(inside, found, -1)


def allowed_of(row_seg_ref, col_seg_ref):
    width = row_seg_ref.shape[1]
    cols = jnp.transpose(jnp.broadcast_to(col_seg_ref[...], (width, width)))
    return cols == row_seg_ref[...]


def stats_kernel(flag_ref, rows_ref, kv_ref, row_seg_ref, col_seg_ref, out_ref):
    @pl.when(flag_ref[0] == 0)
    def _():
        out_ref[0] = jnp.full(out_ref.shape[1:], NEG, jnp.float32)
        out_ref[1] = jnp.zeros(out_ref.shape[1:], jnp.float32)
        out_ref[2] = jnp.zeros(out_ref.shape[1:], jnp.float32)

    @pl.when(flag_ref[0] != 0)
    def _():
        allowed = allowed_of(row_seg_ref, col_seg_ref)
        scale = HEAD_DIM ** (-0.5)
        for h in range(HEADS):
            cols = slice(h * HEAD_DIM, (h + 1) * HEAD_DIM)
            query = rows_ref[0, :, cols]
            grad = rows_ref[1, :, cols]
            scores = lax.dot_general(
                kv_ref[0, :, cols], query, NT, preferred_element_type=jnp.float32
            ) * scale
            scores = jnp.where(allowed, scores, NEG)
            maximum = jnp.max(scores, axis=0, keepdims=True)
            probs = jnp.where(allowed, jnp.exp(scores - maximum), 0.0)
            dprobs = lax.dot_general(
                kv_ref[1, :, cols], grad, NT, preferred_element_type=jnp.float32
            )
            out_ref[0, h : h + 1, :] = maximum
            out_ref[1, h : h + 1, :] = jnp.sum(probs, axis=0, keepdims=True)
            out_ref[2, h : h + 1, :] = jnp.sum(probs * dprobs, axis=0, keepdims=True)


def grad_kernel(flag_ref, rows_ref, final_ref, kv_ref, row_seg_ref, col_seg_ref, gq_ref, gkv_ref):

    @pl.when(flag_ref[0] == 0)
    def _():
        gq_ref[...] = jnp.zeros(gq_ref.shape, gq_ref.dtype)
        gkv_ref[...] = jnp.zeros(gkv_ref.shape, gkv_ref.dtype)

    @pl.when(flag_ref[0] != 0)
    def _():
        allowed = allowed_of(row_seg_ref, col_seg_ref)
        scale = HEAD_DIM ** (-0.5)
        for h in range(HEADS):
            cols = slice(h * HEAD_DIM, (h + 1) * HEAD_DIM)
            query = rows_ref[0, :, cols]
            grad = rows_ref[1, :, cols]
            key = kv_ref[0, :, cols]
            log_total = final_ref[0, h : h + 1, :]
            delta = final_ref[1, h : h + 1, :]
            scores = lax.dot_general(key, query, NT, preferred_element_type=jnp.float32) * scale
            probs = jnp.where(allowed, jnp.exp(scores - log_total), 0.0)
            dprobs = lax.dot_general(
                kv_ref[1, :, cols], grad, NT, preferred_element_type=jnp.float32
            )
            dscores = jnp.where(allowed, probs * (dprobs - delta), 0.0)
            probs_low = probs.astype(jnp.bfloat16)
            dscores_low = dscores.astype(jnp.bfloat16)
            gk = jnp.dot(dscores_low, query, preferred_element_type=jnp.float32) * scale
            gv = jnp.dot(probs_low, grad, preferred_element_type=jnp.float32)
            gq = lax.dot_general(dscores_low, key, TN, preferred_element_type=jnp.float32) * scale
            gq_ref[:, cols] = gq.astype(gq_ref.dtype)
            gkv_ref[0, :, cols] = gk.astype(gkv_ref.dtype)
            gkv_ref[1, :, cols] = gv.astype(gkv_ref.dtype)


def vmem_specs(count):
    return [pl.BlockSpec(memory_space=pltpu.SMEM)] + [
        pl.BlockSpec(memory_space=pltpu.VMEM) for _ in range(count)
    ]


def pair_statistics(flag, rows, kv, row_segments, col_segments):
    return pl.pallas_call(
        stats_kernel,
        out_shape=jax.ShapeDtypeStruct((3, HEADS, rows.shape[1]), jnp.float32),
        in_specs=vmem_specs(4),
    )(flag, rows, kv, row_segments[None, :], col_segments[None, :])


def pair_gradients(flag, rows, final, kv, row_segments, col_segments, out_dtype):
    return pl.pallas_call(
        grad_kernel,
        out_shape=(
            jax.ShapeDtypeStruct(rows.shape[1:], out_dtype),
            jax.ShapeDtypeStruct(kv.shape, out_dtype),
        ),
        in_specs=vmem_specs(5),
    )(flag, rows, final, kv, row_segments[None, :], col_segments[None, :])


def merge_statistics(first, second):
    maximum = jnp.maximum(first[0], second[0])
    scale_one = jnp.exp(first[0] - maximum)
    scale_two = jnp.exp(second[0] - maximum)
    return (
        maximum,
        first[1] * scale_one + second[1] * scale_two,
        first[2] * scale_one + second[2] * scale_two,
    )


def finalize(statistics):
    return (statistics[0] + jnp.log(statistics[1]), statistics[2] / statistics[1])


def on_device(queries, keys, values, grad_out, offsets):
    axis = ("grp", "ctx")
    block_len = queries.shape[0]
    device_count = lax.axis_size(axis)
    slab_len = device_count * block_len
    device_index = lax.axis_index(axis)
    own_positions = device_index * block_len + jnp.arange(block_len, dtype=jnp.int32)
    own_segments = segments(offsets, own_positions, slab_len)
    rows = jnp.stack([queries, grad_out])
    kv = jnp.stack([keys, values])
    distances = [d for d in range(1, MAXP + 1)] + [-d for d in range(1, MAXP + 1)]
    always = jnp.ones((1,), jnp.int32)

    received = {}
    for distance in distances:
        far_kv = shifted(kv, axis, -distance)
        far_segments = segments(offsets, own_positions + distance * block_len, slab_len)
        shared = jnp.any(far_segments[:, None] == own_segments[None, :])
        received[distance] = (far_kv, far_segments, shared)

    own = pair_statistics(always, rows, kv, own_segments, own_segments)
    row_stats = (own[0], own[1], own[2])
    for distance in distances:
        far_kv, far_segments, shared = received[distance]
        flag = shared.astype(jnp.int32).reshape(1)
        partial = pair_statistics(flag, rows, far_kv, own_segments, far_segments)
        row_stats = merge_statistics(row_stats, (partial[0], partial[1], partial[2]))
    log_total, delta_rows = finalize(row_stats)
    final_stats = jnp.stack([log_total, delta_rows])

    grad_query, grad_kv = pair_gradients(
        always, rows, final_stats, kv, own_segments, own_segments, jnp.float32
    )
    for distance in distances:
        far_kv, far_segments, shared = received[distance]
        flag = shared.astype(jnp.int32).reshape(1)
        far_gq, far_gkv = pair_gradients(
            flag, rows, final_stats, far_kv, own_segments, far_segments, jnp.bfloat16
        )
        grad_query = grad_query + far_gq.astype(jnp.float32)
        back_kv = shifted(far_gkv, axis, distance)
        grad_kv = grad_kv + back_kv.astype(jnp.float32)
    return (
        grad_query.astype(jnp.bfloat16),
        grad_kv[0].astype(jnp.bfloat16),
        grad_kv[1].astype(jnp.bfloat16),
    )


def solution(mesh):
    placed = (
        P(("grp", "ctx"), None),
        P(("grp", "ctx"), None),
        P(("grp", "ctx"), None),
        P(("grp", "ctx"), None),
        P(),
    )
    return jax.shard_map(
        on_device,
        mesh=mesh,
        in_specs=placed,
        out_specs=(P(("grp", "ctx"), None), P(("grp", "ctx"), None), P(("grp", "ctx"), None)),
        check_vma=False,
    )
```

```python
import functools

import jax
import jax.numpy as jnp
from jax import lax
from jax.experimental import pallas as pl
from jax.experimental.pallas import tpu as pltpu
from jax.sharding import PartitionSpec as P

HEADS = 14
HEAD_DIM = 128
MAXP = 3


NEG = -1e30


NT = (((1,), (1,)), ((), ()))
TN = (((0,), (0,)), ((), ()))


def shifted(value, axis, by):
    peers = lax.axis_size(axis)
    pairs = [(i, i + by) for i in range(peers) if 0 <= i + by < peers]
    return lax.ppermute(value, axis, pairs)


def segments(offsets, positions, slab_len):
    found = jnp.sum((offsets[None, :] <= positions[:, None]).astype(jnp.int32), axis=1) - 1
    inside = (positions >= 0) & (positions < slab_len)
    return jnp.where(inside, found, -1)


def allowed_of(row_seg_ref, col_seg_ref):
    width = row_seg_ref.shape[1]
    cols = jnp.transpose(jnp.broadcast_to(col_seg_ref[...], (width, width)))
    return cols == row_seg_ref[...]


def stats_kernel(flag_ref, rows_ref, kv_ref, row_seg_ref, col_seg_ref, out_ref):
    @pl.when(flag_ref[0] == 0)
    def _():
        out_ref[0] = jnp.full(out_ref.shape[1:], NEG, jnp.float32)
        out_ref[1] = jnp.zeros(out_ref.shape[1:], jnp.float32)
        out_ref[2] = jnp.zeros(out_ref.shape[1:], jnp.float32)

    @pl.when(flag_ref[0] != 0)
    def _():
        allowed = allowed_of(row_seg_ref, col_seg_ref)
        scale = HEAD_DIM ** (-0.5)
        for h in range(HEADS):
            cols = slice(h * HEAD_DIM, (h + 1) * HEAD_DIM)
            query = rows_ref[0, :, cols]
            grad = rows_ref[1, :, cols]
            scores = lax.dot_general(
                kv_ref[0, :, cols], query, NT, preferred_element_type=jnp.float32
            ) * scale
            scores = jnp.where(allowed, scores, NEG)
            maximum = jnp.max(scores, axis=0, keepdims=True)
            probs = jnp.where(allowed, jnp.exp(scores - maximum), 0.0)
            dprobs = lax.dot_general(
                kv_ref[1, :, cols], grad, NT, preferred_element_type=jnp.float32
            )
            out_ref[0, h : h + 1, :] = maximum
            out_ref[1, h : h + 1, :] = jnp.sum(probs, axis=0, keepdims=True)
            out_ref[2, h : h + 1, :] = jnp.sum(probs * dprobs, axis=0, keepdims=True)


def grad_kernel(flag_ref, rows_ref, final_ref, kv_ref, row_seg_ref, col_seg_ref, gq_ref, gkv_ref):

    @pl.when(flag_ref[0] == 0)
    def _():
        gq_ref[...] = jnp.zeros(gq_ref.shape, gq_ref.dtype)
        gkv_ref[...] = jnp.zeros(gkv_ref.shape, gkv_ref.dtype)

    @pl.when(flag_ref[0] != 0)
    def _():
        allowed = allowed_of(row_seg_ref, col_seg_ref)
        scale = HEAD_DIM ** (-0.5)
        for h in range(HEADS):
            cols = slice(h * HEAD_DIM, (h + 1) * HEAD_DIM)
            query = rows_ref[0, :, cols]
            grad = rows_ref[1, :, cols]
            key = kv_ref[0, :, cols]
            log_total = final_ref[0, h : h + 1, :]
            delta = final_ref[1, h : h + 1, :]
            scores = lax.dot_general(key, query, NT, preferred_element_type=jnp.float32) * scale
            probs = jnp.where(allowed, jnp.exp(scores - log_total), 0.0)
            dprobs = lax.dot_general(
                kv_ref[1, :, cols], grad, NT, preferred_element_type=jnp.float32
            )
            dscores = jnp.where(allowed, probs * (dprobs - delta), 0.0)
            probs_low = probs.astype(jnp.bfloat16)
            dscores_low = dscores.astype(jnp.bfloat16)
            gk = jnp.dot(dscores_low, query, preferred_element_type=jnp.float32) * scale
            gv = jnp.dot(probs_low, grad, preferred_element_type=jnp.float32)
            gq = lax.dot_general(dscores_low, key, TN, preferred_element_type=jnp.float32) * scale
            gq_ref[:, cols] = gq.astype(gq_ref.dtype)
            gkv_ref[0, :, cols] = gk.astype(gkv_ref.dtype)
            gkv_ref[1, :, cols] = gv.astype(gkv_ref.dtype)


def vmem_specs(count):
    return [pl.BlockSpec(memory_space=pltpu.SMEM)] + [
        pl.BlockSpec(memory_space=pltpu.VMEM) for _ in range(count)
    ]


def pair_statistics(flag, rows, kv, row_segments, col_segments):
    return pl.pallas_call(
        stats_kernel,
        out_shape=jax.ShapeDtypeStruct((3, HEADS, rows.shape[1]), jnp.float32),
        in_specs=vmem_specs(4),
    )(flag, rows, kv, row_segments[None, :], col_segments[None, :])


def pair_gradients(flag, rows, final, kv, row_segments, col_segments, out_dtype):
    return pl.pallas_call(
        grad_kernel,
        out_shape=(
            jax.ShapeDtypeStruct(rows.shape[1:], out_dtype),
            jax.ShapeDtypeStruct(kv.shape, out_dtype),
        ),
        in_specs=vmem_specs(5),
    )(flag, rows, final, kv, row_segments[None, :], col_segments[None, :])


def merge_statistics(first, second):
    maximum = jnp.maximum(first[0], second[0])
    scale_one = jnp.exp(first[0] - maximum)
    scale_two = jnp.exp(second[0] - maximum)
    return (
        maximum,
        first[1] * scale_one + second[1] * scale_two,
        first[2] * scale_one + second[2] * scale_two,
    )


def finalize(statistics):
    return (statistics[0] + jnp.log(statistics[1]), statistics[2] / statistics[1])


def on_device(queries, keys, values, grad_out, offsets):
    axis = ("grp", "ctx")
    block_len = queries.shape[0]
    device_count = lax.axis_size(axis)
    slab_len = device_count * block_len
    device_index = lax.axis_index(axis)
    own_positions = device_index * block_len + jnp.arange(block_len, dtype=jnp.int32)
    own_segments = segments(offsets, own_positions, slab_len)
    rows = jnp.stack([queries, grad_out])
    kv = jnp.stack([keys, values])
    distances = [d for d in range(1, MAXP + 1)] + [-d for d in range(1, MAXP + 1)]
    always = jnp.ones((1,), jnp.int32)

    halo = {}
    up, down = kv, kv
    for distance in range(1, MAXP + 1):
        up = shifted(up, axis, -1)
        down = shifted(down, axis, 1)
        halo[distance], halo[-distance] = up, down
    received = {}
    for distance in distances:
        far_kv = halo[distance]
        far_segments = segments(offsets, own_positions + distance * block_len, slab_len)
        shared = jnp.any(far_segments[:, None] == own_segments[None, :])
        received[distance] = (far_kv, far_segments, shared)

    own = pair_statistics(always, rows, kv, own_segments, own_segments)
    row_stats = (own[0], own[1], own[2])
    for distance in distances:
        far_kv, far_segments, shared = received[distance]
        flag = shared.astype(jnp.int32).reshape(1)
        partial = pair_statistics(flag, rows, far_kv, own_segments, far_segments)
        row_stats = merge_statistics(row_stats, (partial[0], partial[1], partial[2]))
    log_total, delta_rows = finalize(row_stats)
    final_stats = jnp.stack([log_total, delta_rows])

    grad_query, grad_kv = pair_gradients(
        always, rows, final_stats, kv, own_segments, own_segments, jnp.float32
    )
    for distance in distances:
        far_kv, far_segments, shared = received[distance]
        flag = shared.astype(jnp.int32).reshape(1)
        far_gq, far_gkv = pair_gradients(
            flag, rows, final_stats, far_kv, own_segments, far_segments, jnp.bfloat16
        )
        grad_query = grad_query + far_gq.astype(jnp.float32)
        back_kv = shifted(far_gkv, axis, distance)
        grad_kv = grad_kv + back_kv.astype(jnp.float32)
    return (
        grad_query.astype(jnp.bfloat16),
        grad_kv[0].astype(jnp.bfloat16),
        grad_kv[1].astype(jnp.bfloat16),
    )


def solution(mesh):
    placed = (
        P(("grp", "ctx"), None),
        P(("grp", "ctx"), None),
        P(("grp", "ctx"), None),
        P(("grp", "ctx"), None),
        P(),
    )
    return jax.shard_map(
        on_device,
        mesh=mesh,
        in_specs=placed,
        out_specs=(P(("grp", "ctx"), None), P(("grp", "ctx"), None), P(("grp", "ctx"), None)),
        check_vma=False,
    )
```

```python
import functools

import jax
import jax.numpy as jnp
from jax import lax
from jax.experimental import pallas as pl
from jax.experimental.pallas import tpu as pltpu
from jax.sharding import PartitionSpec as P

HEADS = 14
HEAD_DIM = 128
MAXP = 3


NEG = -1e30


NT = (((1,), (1,)), ((), ()))
TN = (((0,), (0,)), ((), ()))


def shifted(value, axis, by):
    peers = lax.axis_size(axis)
    pairs = [(i, i + by) for i in range(peers) if 0 <= i + by < peers]
    return lax.ppermute(value, axis, pairs)


def segments(offsets, positions, slab_len):
    found = jnp.sum((offsets[None, :] <= positions[:, None]).astype(jnp.int32), axis=1) - 1
    inside = (positions >= 0) & (positions < slab_len)
    return jnp.where(inside, found, -1)


def allowed_of(row_seg_ref, col_seg_ref):
    width = row_seg_ref.shape[1]
    cols = jnp.transpose(jnp.broadcast_to(col_seg_ref[...], (width, width)))
    return cols == row_seg_ref[...]


def stats_kernel(flag_ref, rows_ref, kv_ref, row_seg_ref, col_seg_ref, out_ref):
    @pl.when(flag_ref[0] == 0)
    def _():
        out_ref[0] = jnp.full(out_ref.shape[1:], NEG, jnp.float32)
        out_ref[1] = jnp.zeros(out_ref.shape[1:], jnp.float32)
        out_ref[2] = jnp.zeros(out_ref.shape[1:], jnp.float32)

    @pl.when(flag_ref[0] != 0)
    def _():
        allowed = allowed_of(row_seg_ref, col_seg_ref)
        scale = HEAD_DIM ** (-0.5)
        for h in range(HEADS):
            cols = slice(h * HEAD_DIM, (h + 1) * HEAD_DIM)
            query = rows_ref[0, :, cols]
            grad = rows_ref[1, :, cols]
            scores = lax.dot_general(
                kv_ref[0, :, cols], query, NT, preferred_element_type=jnp.float32
            ) * scale
            scores = jnp.where(allowed, scores, NEG)
            maximum = jnp.max(scores, axis=0, keepdims=True)
            probs = jnp.where(allowed, jnp.exp(scores - maximum), 0.0)
            dprobs = lax.dot_general(
                kv_ref[1, :, cols], grad, NT, preferred_element_type=jnp.float32
            )
            out_ref[0, h : h + 1, :] = maximum
            out_ref[1, h : h + 1, :] = jnp.sum(probs, axis=0, keepdims=True)
            out_ref[2, h : h + 1, :] = jnp.sum(probs * dprobs, axis=0, keepdims=True)


def grad_kernel(flag_ref, rows_ref, final_ref, kv_ref, row_seg_ref, col_seg_ref, gq_ref, gkv_ref):

    @pl.when(flag_ref[0] == 0)
    def _():
        gq_ref[...] = jnp.zeros(gq_ref.shape, gq_ref.dtype)
        gkv_ref[...] = jnp.zeros(gkv_ref.shape, gkv_ref.dtype)

    @pl.when(flag_ref[0] != 0)
    def _():
        allowed = allowed_of(row_seg_ref, col_seg_ref)
        scale = HEAD_DIM ** (-0.5)
        for h in range(HEADS):
            cols = slice(h * HEAD_DIM, (h + 1) * HEAD_DIM)
            query = rows_ref[0, :, cols]
            grad = rows_ref[1, :, cols]
            key = kv_ref[0, :, cols]
            log_total = final_ref[0, h : h + 1, :]
            delta = final_ref[1, h : h + 1, :]
            scores = lax.dot_general(key, query, NT, preferred_element_type=jnp.float32) * scale
            probs = jnp.where(allowed, jnp.exp(scores - log_total), 0.0)
            dprobs = lax.dot_general(
                kv_ref[1, :, cols], grad, NT, preferred_element_type=jnp.float32
            )
            dscores = jnp.where(allowed, probs * (dprobs - delta), 0.0)
            probs_low = probs.astype(jnp.bfloat16)
            dscores_low = dscores.astype(jnp.bfloat16)
            gk = jnp.dot(dscores_low, query, preferred_element_type=jnp.float32) * scale
            gv = jnp.dot(probs_low, grad, preferred_element_type=jnp.float32)
            gq = lax.dot_general(dscores_low, key, TN, preferred_element_type=jnp.float32) * scale
            gq_ref[:, cols] = gq.astype(gq_ref.dtype)
            gkv_ref[0, :, cols] = gk.astype(gkv_ref.dtype)
            gkv_ref[1, :, cols] = gv.astype(gkv_ref.dtype)


def vmem_specs(count):
    return [pl.BlockSpec(memory_space=pltpu.SMEM)] + [
        pl.BlockSpec(memory_space=pltpu.VMEM) for _ in range(count)
    ]


def pair_statistics(flag, rows, kv, row_segments, col_segments):
    return pl.pallas_call(
        stats_kernel,
        out_shape=jax.ShapeDtypeStruct((3, HEADS, rows.shape[1]), jnp.float32),
        in_specs=vmem_specs(4),
    )(flag, rows, kv, row_segments[None, :], col_segments[None, :])


def pair_gradients(flag, rows, final, kv, row_segments, col_segments, out_dtype):
    return pl.pallas_call(
        grad_kernel,
        out_shape=(
            jax.ShapeDtypeStruct(rows.shape[1:], out_dtype),
            jax.ShapeDtypeStruct(kv.shape, out_dtype),
        ),
        in_specs=vmem_specs(5),
    )(flag, rows, final, kv, row_segments[None, :], col_segments[None, :])


def merge_statistics(first, second):
    maximum = jnp.maximum(first[0], second[0])
    scale_one = jnp.exp(first[0] - maximum)
    scale_two = jnp.exp(second[0] - maximum)
    return (
        maximum,
        first[1] * scale_one + second[1] * scale_two,
        first[2] * scale_one + second[2] * scale_two,
    )


def finalize(statistics):
    return (statistics[0] + jnp.log(statistics[1]), statistics[2] / statistics[1])


def on_device(queries, keys, values, grad_out, offsets):
    axis = ("grp", "ctx")
    block_len = queries.shape[0]
    device_count = lax.axis_size(axis)
    slab_len = device_count * block_len
    device_index = lax.axis_index(axis)
    own_positions = device_index * block_len + jnp.arange(block_len, dtype=jnp.int32)
    own_segments = segments(offsets, own_positions, slab_len)
    rows = jnp.stack([queries, grad_out])
    kv = jnp.stack([keys, values])
    distances = [d for d in range(1, MAXP + 1)] + [-d for d in range(1, MAXP + 1)]
    always = jnp.ones((1,), jnp.int32)

    halo = {}
    up, down = kv, kv
    for distance in range(1, MAXP + 1):
        up = shifted(up, axis, -1)
        down = shifted(down, axis, 1)
        halo[distance], halo[-distance] = up, down
    received = {}
    for distance in distances:
        far_kv = halo[distance]
        far_segments = segments(offsets, own_positions + distance * block_len, slab_len)
        shared = jnp.any(far_segments[:, None] == own_segments[None, :])
        received[distance] = (far_kv, far_segments, shared)

    own = pair_statistics(always, rows, kv, own_segments, own_segments)
    row_stats = (own[0], own[1], own[2])
    for distance in distances:
        far_kv, far_segments, shared = received[distance]
        flag = shared.astype(jnp.int32).reshape(1)
        partial = pair_statistics(flag, rows, far_kv, own_segments, far_segments)
        row_stats = merge_statistics(row_stats, (partial[0], partial[1], partial[2]))
    log_total, delta_rows = finalize(row_stats)
    final_stats = jnp.stack([log_total, delta_rows])

    grad_query, grad_kv = pair_gradients(
        always, rows, final_stats, kv, own_segments, own_segments, jnp.float32
    )
    terms = {}
    for distance in sorted(distances, key=lambda d: (-abs(d), -d)):
        far_kv, far_segments, shared = received[distance]
        flag = shared.astype(jnp.int32).reshape(1)
        far_gq, terms[distance] = pair_gradients(
            flag, rows, final_stats, far_kv, own_segments, far_segments, jnp.bfloat16
        )
        grad_query = grad_query + far_gq.astype(jnp.float32)
    for sign in (1, -1):
        carried = shifted(terms[sign * MAXP], axis, sign).astype(jnp.float32)
        for distance in range(MAXP - 1, 0, -1):
            carried = shifted(carried + terms[sign * distance].astype(jnp.float32), axis, sign)
        grad_kv = grad_kv + carried
    return (
        grad_query.astype(jnp.bfloat16),
        grad_kv[0].astype(jnp.bfloat16),
        grad_kv[1].astype(jnp.bfloat16),
    )


def solution(mesh):
    placed = (
        P(("grp", "ctx"), None),
        P(("grp", "ctx"), None),
        P(("grp", "ctx"), None),
        P(("grp", "ctx"), None),
        P(),
    )
    return jax.shard_map(
        on_device,
        mesh=mesh,
        in_specs=placed,
        out_specs=(P(("grp", "ctx"), None), P(("grp", "ctx"), None), P(("grp", "ctx"), None)),
        check_vma=False,
    )
```

```python
import functools

import jax
import jax.numpy as jnp
from jax import lax
from jax.experimental import pallas as pl
from jax.experimental.pallas import tpu as pltpu
from jax.sharding import PartitionSpec as P

HEADS = 14
HEAD_DIM = 128
MAXP = 3


NEG = -1e30


NT = (((1,), (1,)), ((), ()))
TN = (((0,), (0,)), ((), ()))


def shifted(value, axis, by):
    peers = lax.axis_size(axis)
    pairs = [(i, i + by) for i in range(peers) if 0 <= i + by < peers]
    return lax.ppermute(value, axis, pairs)


def segments(offsets, positions, slab_len):
    found = jnp.sum((offsets[None, :] <= positions[:, None]).astype(jnp.int32), axis=1) - 1
    inside = (positions >= 0) & (positions < slab_len)
    return jnp.where(inside, found, -1)


def allowed_of(row_seg_ref, col_seg_ref):
    width = row_seg_ref.shape[1]
    cols = jnp.transpose(jnp.broadcast_to(col_seg_ref[...], (width, width)))
    return cols == row_seg_ref[...]


def stats_kernel(flag_ref, rows_ref, kv_ref, row_seg_ref, col_seg_ref, out_ref):
    @pl.when(flag_ref[0] == 0)
    def _():
        out_ref[0] = jnp.full(out_ref.shape[1:], NEG, jnp.float32)
        out_ref[1] = jnp.zeros(out_ref.shape[1:], jnp.float32)
        out_ref[2] = jnp.zeros(out_ref.shape[1:], jnp.float32)

    @pl.when(flag_ref[0] != 0)
    def _():
        allowed = allowed_of(row_seg_ref, col_seg_ref)
        scale = HEAD_DIM ** (-0.5)
        for h in range(HEADS):
            cols = slice(h * HEAD_DIM, (h + 1) * HEAD_DIM)
            query = rows_ref[0, :, cols]
            grad = rows_ref[1, :, cols]
            scores = lax.dot_general(
                kv_ref[0, :, cols], query, NT, preferred_element_type=jnp.float32
            ) * scale
            scores = jnp.where(allowed, scores, NEG)
            maximum = jnp.max(scores, axis=0, keepdims=True)
            probs = jnp.where(allowed, jnp.exp(scores - maximum), 0.0)
            dprobs = lax.dot_general(
                kv_ref[1, :, cols], grad, NT, preferred_element_type=jnp.float32
            )
            out_ref[0, h : h + 1, :] = maximum
            out_ref[1, h : h + 1, :] = jnp.sum(probs, axis=0, keepdims=True)
            out_ref[2, h : h + 1, :] = jnp.sum(probs * dprobs, axis=0, keepdims=True)


def grad_kernel(flag_ref, rows_ref, final_ref, kv_ref, row_seg_ref, col_seg_ref, gq_ref, gkv_ref):

    @pl.when(flag_ref[0] == 0)
    def _():
        gq_ref[...] = jnp.zeros(gq_ref.shape, gq_ref.dtype)
        gkv_ref[...] = jnp.zeros(gkv_ref.shape, gkv_ref.dtype)

    @pl.when(flag_ref[0] != 0)
    def _():
        allowed = allowed_of(row_seg_ref, col_seg_ref)
        scale = HEAD_DIM ** (-0.5)
        for h in range(HEADS):
            cols = slice(h * HEAD_DIM, (h + 1) * HEAD_DIM)
            query = rows_ref[0, :, cols]
            grad = rows_ref[1, :, cols]
            key = kv_ref[0, :, cols]
            log_total = final_ref[0, h : h + 1, :]
            delta = final_ref[1, h : h + 1, :]
            scores = lax.dot_general(key, query, NT, preferred_element_type=jnp.float32) * scale
            probs = jnp.where(allowed, jnp.exp(scores - log_total), 0.0)
            dprobs = lax.dot_general(
                kv_ref[1, :, cols], grad, NT, preferred_element_type=jnp.float32
            )
            dscores = jnp.where(allowed, probs * (dprobs - delta), 0.0)
            probs_low = probs.astype(jnp.bfloat16)
            dscores_low = dscores.astype(jnp.bfloat16)
            gk = jnp.dot(dscores_low, query, preferred_element_type=jnp.float32) * scale
            gv = jnp.dot(probs_low, grad, preferred_element_type=jnp.float32)
            gq = lax.dot_general(dscores_low, key, TN, preferred_element_type=jnp.float32) * scale
            gq_ref[:, cols] = gq.astype(gq_ref.dtype)
            gkv_ref[0, :, cols] = gk.astype(gkv_ref.dtype)
            gkv_ref[1, :, cols] = gv.astype(gkv_ref.dtype)


def vmem_specs(count):
    return [pl.BlockSpec(memory_space=pltpu.SMEM)] + [
        pl.BlockSpec(memory_space=pltpu.VMEM) for _ in range(count)
    ]


def pair_statistics(flag, rows, kv, row_segments, col_segments):
    return pl.pallas_call(
        stats_kernel,
        out_shape=jax.ShapeDtypeStruct((3, HEADS, rows.shape[1]), jnp.float32),
        in_specs=vmem_specs(4),
    )(flag, rows, kv, row_segments[None, :], col_segments[None, :])


def pair_gradients(flag, rows, final, kv, row_segments, col_segments, out_dtype):
    return pl.pallas_call(
        grad_kernel,
        out_shape=(
            jax.ShapeDtypeStruct(rows.shape[1:], out_dtype),
            jax.ShapeDtypeStruct(kv.shape, out_dtype),
        ),
        in_specs=vmem_specs(5),
    )(flag, rows, final, kv, row_segments[None, :], col_segments[None, :])


def merge_statistics(first, second):
    maximum = jnp.maximum(first[0], second[0])
    scale_one = jnp.exp(first[0] - maximum)
    scale_two = jnp.exp(second[0] - maximum)
    return (
        maximum,
        first[1] * scale_one + second[1] * scale_two,
        first[2] * scale_one + second[2] * scale_two,
    )


def finalize(statistics):
    return (statistics[0] + jnp.log(statistics[1]), statistics[2] / statistics[1])


def on_device(queries, keys, values, grad_out, offsets):
    axis = ("grp", "ctx")
    block_len = queries.shape[0]
    device_count = lax.axis_size(axis)
    slab_len = device_count * block_len
    device_index = lax.axis_index(axis)
    own_positions = device_index * block_len + jnp.arange(block_len, dtype=jnp.int32)
    own_segments = segments(offsets, own_positions, slab_len)
    rows = jnp.stack([queries, grad_out])
    kv = jnp.stack([keys, values])
    distances = [d for d in range(1, MAXP + 1)] + [-d for d in range(1, MAXP + 1)]
    always = jnp.ones((1,), jnp.int32)

    halo = {}
    up, down = kv, kv
    for distance in range(1, MAXP + 1):
        up = shifted(up, axis, -1)
        down = shifted(down, axis, 1)
        halo[distance], halo[-distance] = up, down
    received = {}
    for distance in distances:
        far_kv = halo[distance]
        far_segments = segments(offsets, own_positions + distance * block_len, slab_len)
        shared = jnp.any(far_segments[:, None] == own_segments[None, :])
        received[distance] = (far_kv, far_segments, shared)

    own = pair_statistics(always, rows, kv, own_segments, own_segments)
    row_stats = (own[0], own[1], own[2])
    for distance in distances:
        far_kv, far_segments, shared = received[distance]
        flag = shared.astype(jnp.int32).reshape(1)
        partial = pair_statistics(flag, rows, far_kv, own_segments, far_segments)
        row_stats = merge_statistics(row_stats, (partial[0], partial[1], partial[2]))
    log_total, delta_rows = finalize(row_stats)
    final_stats = jnp.stack([log_total, delta_rows])

    grad_query, grad_kv = pair_gradients(
        always, rows, final_stats, kv, own_segments, own_segments, jnp.float32
    )
    terms = {}
    for distance in sorted(distances, key=lambda d: (-abs(d), -d)):
        far_kv, far_segments, shared = received[distance]
        flag = shared.astype(jnp.int32).reshape(1)
        far_gq, terms[distance] = pair_gradients(
            flag, rows, final_stats, far_kv, own_segments, far_segments, jnp.bfloat16
        )
        grad_query = grad_query + far_gq.astype(jnp.float32)
    for sign in (1, -1):
        carried = shifted(terms[sign * MAXP], axis, sign)
        for distance in range(MAXP - 1, 0, -1):
            partial = carried.astype(jnp.float32) + terms[sign * distance].astype(jnp.float32)
            carried = shifted(partial.astype(jnp.bfloat16), axis, sign)
        grad_kv = grad_kv + carried.astype(jnp.float32)
    return (
        grad_query.astype(jnp.bfloat16),
        grad_kv[0].astype(jnp.bfloat16),
        grad_kv[1].astype(jnp.bfloat16),
    )


def solution(mesh):
    placed = (
        P(("grp", "ctx"), None),
        P(("grp", "ctx"), None),
        P(("grp", "ctx"), None),
        P(("grp", "ctx"), None),
        P(),
    )
    return jax.shard_map(
        on_device,
        mesh=mesh,
        in_specs=placed,
        out_specs=(P(("grp", "ctx"), None), P(("grp", "ctx"), None), P(("grp", "ctx"), None)),
        check_vma=False,
    )
```

```python
import functools

import jax
import jax.numpy as jnp
from jax import lax
from jax.experimental import pallas as pl
from jax.experimental.pallas import tpu as pltpu
from jax.sharding import PartitionSpec as P

HEADS = 14
HEAD_DIM = 128
MAXP = 3


NEG = -1e30


NT = (((1,), (1,)), ((), ()))
TN = (((0,), (0,)), ((), ()))


def shifted(value, axis, by):
    peers = lax.axis_size(axis)
    pairs = [(i, i + by) for i in range(peers) if 0 <= i + by < peers]
    return lax.ppermute(value, axis, pairs)


def segments(offsets, positions, slab_len):
    found = jnp.sum((offsets[None, :] <= positions[:, None]).astype(jnp.int32), axis=1) - 1
    inside = (positions >= 0) & (positions < slab_len)
    return jnp.where(inside, found, -1)


def allowed_of(row_seg_ref, col_seg_ref):
    width = row_seg_ref.shape[1]
    cols = jnp.transpose(jnp.broadcast_to(col_seg_ref[...], (width, width)))
    return cols == row_seg_ref[...]


def fetch(rows_hbm, kv_hbm, rows_ref, kv_ref, sems):
    copies = [
        pltpu.make_async_copy(rows_hbm, rows_ref, sems.at[0]),
        pltpu.make_async_copy(kv_hbm, kv_ref, sems.at[1]),
    ]
    for copy in copies:
        copy.start()
    for copy in copies:
        copy.wait()


def stats_kernel(
    flag_ref, rows_hbm, kv_hbm, row_seg_ref, col_seg_ref, out_ref, rows_ref, kv_ref, sems
):
    @pl.when(flag_ref[0] == 0)
    def _():
        out_ref[0] = jnp.full(out_ref.shape[1:], NEG, jnp.float32)
        out_ref[1] = jnp.zeros(out_ref.shape[1:], jnp.float32)
        out_ref[2] = jnp.zeros(out_ref.shape[1:], jnp.float32)

    @pl.when(flag_ref[0] != 0)
    def _():
        fetch(rows_hbm, kv_hbm, rows_ref, kv_ref, sems)
        allowed = allowed_of(row_seg_ref, col_seg_ref)
        scale = HEAD_DIM ** (-0.5)
        for h in range(HEADS):
            cols = slice(h * HEAD_DIM, (h + 1) * HEAD_DIM)
            query = rows_ref[0, :, cols]
            grad = rows_ref[1, :, cols]
            scores = lax.dot_general(
                kv_ref[0, :, cols], query, NT, preferred_element_type=jnp.float32
            ) * scale
            scores = jnp.where(allowed, scores, NEG)
            maximum = jnp.max(scores, axis=0, keepdims=True)
            probs = jnp.where(allowed, jnp.exp(scores - maximum), 0.0)
            dprobs = lax.dot_general(
                kv_ref[1, :, cols], grad, NT, preferred_element_type=jnp.float32
            )
            out_ref[0, h : h + 1, :] = maximum
            out_ref[1, h : h + 1, :] = jnp.sum(probs, axis=0, keepdims=True)
            out_ref[2, h : h + 1, :] = jnp.sum(probs * dprobs, axis=0, keepdims=True)


def grad_kernel(
    flag_ref, rows_hbm, final_ref, kv_hbm, row_seg_ref, col_seg_ref, gq_ref, gkv_ref,
    rows_ref, kv_ref, sems,
):

    @pl.when(flag_ref[0] == 0)
    def _():
        gq_ref[...] = jnp.zeros(gq_ref.shape, gq_ref.dtype)
        gkv_ref[...] = jnp.zeros(gkv_ref.shape, gkv_ref.dtype)

    @pl.when(flag_ref[0] != 0)
    def _():
        fetch(rows_hbm, kv_hbm, rows_ref, kv_ref, sems)
        allowed = allowed_of(row_seg_ref, col_seg_ref)
        scale = HEAD_DIM ** (-0.5)
        for h in range(HEADS):
            cols = slice(h * HEAD_DIM, (h + 1) * HEAD_DIM)
            query = rows_ref[0, :, cols]
            grad = rows_ref[1, :, cols]
            key = kv_ref[0, :, cols]
            log_total = final_ref[0, h : h + 1, :]
            delta = final_ref[1, h : h + 1, :]
            scores = lax.dot_general(key, query, NT, preferred_element_type=jnp.float32) * scale
            probs = jnp.where(allowed, jnp.exp(scores - log_total), 0.0)
            dprobs = lax.dot_general(
                kv_ref[1, :, cols], grad, NT, preferred_element_type=jnp.float32
            )
            dscores = jnp.where(allowed, probs * (dprobs - delta), 0.0)
            probs_low = probs.astype(jnp.bfloat16)
            dscores_low = dscores.astype(jnp.bfloat16)
            gk = jnp.dot(dscores_low, query, preferred_element_type=jnp.float32) * scale
            gv = jnp.dot(probs_low, grad, preferred_element_type=jnp.float32)
            gq = lax.dot_general(dscores_low, key, TN, preferred_element_type=jnp.float32) * scale
            gq_ref[:, cols] = gq.astype(gq_ref.dtype)
            gkv_ref[0, :, cols] = gk.astype(gkv_ref.dtype)
            gkv_ref[1, :, cols] = gv.astype(gkv_ref.dtype)


def memory_specs(*spaces):
    return [pl.BlockSpec(memory_space=space) for space in spaces]


def scratch_for(rows, kv):
    return [
        pltpu.VMEM(rows.shape, rows.dtype),
        pltpu.VMEM(kv.shape, kv.dtype),
        pltpu.SemaphoreType.DMA((2,)),
    ]


def pair_statistics(flag, rows, kv, row_segments, col_segments):
    vmem, anywhere = pltpu.VMEM, pl.ANY
    return pl.pallas_call(
        stats_kernel,
        out_shape=jax.ShapeDtypeStruct((3, HEADS, rows.shape[1]), jnp.float32),
        in_specs=memory_specs(pltpu.SMEM, anywhere, anywhere, vmem, vmem),
        scratch_shapes=scratch_for(rows, kv),
    )(flag, rows, kv, row_segments[None, :], col_segments[None, :])


def pair_gradients(flag, rows, final, kv, row_segments, col_segments, out_dtype):
    vmem, anywhere = pltpu.VMEM, pl.ANY
    return pl.pallas_call(
        grad_kernel,
        out_shape=(
            jax.ShapeDtypeStruct(rows.shape[1:], out_dtype),
            jax.ShapeDtypeStruct(kv.shape, out_dtype),
        ),
        in_specs=memory_specs(pltpu.SMEM, anywhere, vmem, anywhere, vmem, vmem),
        scratch_shapes=scratch_for(rows, kv),
    )(flag, rows, final, kv, row_segments[None, :], col_segments[None, :])


def merge_statistics(first, second):
    maximum = jnp.maximum(first[0], second[0])
    scale_one = jnp.exp(first[0] - maximum)
    scale_two = jnp.exp(second[0] - maximum)
    return (
        maximum,
        first[1] * scale_one + second[1] * scale_two,
        first[2] * scale_one + second[2] * scale_two,
    )


def finalize(statistics):
    return (statistics[0] + jnp.log(statistics[1]), statistics[2] / statistics[1])


def on_device(queries, keys, values, grad_out, offsets):
    axis = ("grp", "ctx")
    block_len = queries.shape[0]
    device_count = lax.axis_size(axis)
    slab_len = device_count * block_len
    device_index = lax.axis_index(axis)
    own_positions = device_index * block_len + jnp.arange(block_len, dtype=jnp.int32)
    own_segments = segments(offsets, own_positions, slab_len)
    rows = jnp.stack([queries, grad_out])
    kv = jnp.stack([keys, values])
    distances = [d for d in range(1, MAXP + 1)] + [-d for d in range(1, MAXP + 1)]
    always = jnp.ones((1,), jnp.int32)

    halo = {}
    up, down = kv, kv
    for distance in range(1, MAXP + 1):
        up = shifted(up, axis, -1)
        down = shifted(down, axis, 1)
        halo[distance], halo[-distance] = up, down
    received = {}
    for distance in distances:
        far_kv = halo[distance]
        far_segments = segments(offsets, own_positions + distance * block_len, slab_len)
        shared = jnp.any(far_segments[:, None] == own_segments[None, :])
        received[distance] = (far_kv, far_segments, shared)

    own = pair_statistics(always, rows, kv, own_segments, own_segments)
    row_stats = (own[0], own[1], own[2])
    for distance in distances:
        far_kv, far_segments, shared = received[distance]
        flag = shared.astype(jnp.int32).reshape(1)
        partial = pair_statistics(flag, rows, far_kv, own_segments, far_segments)
        row_stats = merge_statistics(row_stats, (partial[0], partial[1], partial[2]))
    log_total, delta_rows = finalize(row_stats)
    final_stats = jnp.stack([log_total, delta_rows])

    grad_query, grad_kv = pair_gradients(
        always, rows, final_stats, kv, own_segments, own_segments, jnp.float32
    )
    terms = {}
    for distance in sorted(distances, key=lambda d: (-abs(d), -d)):
        far_kv, far_segments, shared = received[distance]
        flag = shared.astype(jnp.int32).reshape(1)
        far_gq, terms[distance] = pair_gradients(
            flag, rows, final_stats, far_kv, own_segments, far_segments, jnp.bfloat16
        )
        grad_query = grad_query + far_gq.astype(jnp.float32)
    for sign in (1, -1):
        carried = shifted(terms[sign * MAXP], axis, sign)
        for distance in range(MAXP - 1, 0, -1):
            partial = carried.astype(jnp.float32) + terms[sign * distance].astype(jnp.float32)
            carried = shifted(partial.astype(jnp.bfloat16), axis, sign)
        grad_kv = grad_kv + carried.astype(jnp.float32)
    return (
        grad_query.astype(jnp.bfloat16),
        grad_kv[0].astype(jnp.bfloat16),
        grad_kv[1].astype(jnp.bfloat16),
    )


def solution(mesh):
    placed = (
        P(("grp", "ctx"), None),
        P(("grp", "ctx"), None),
        P(("grp", "ctx"), None),
        P(("grp", "ctx"), None),
        P(),
    )
    return jax.shard_map(
        on_device,
        mesh=mesh,
        in_specs=placed,
        out_specs=(P(("grp", "ctx"), None), P(("grp", "ctx"), None), P(("grp", "ctx"), None)),
        check_vma=False,
    )
```

```python
import functools

import jax
import jax.numpy as jnp
from jax import lax
from jax.experimental import pallas as pl
from jax.experimental.pallas import tpu as pltpu
from jax.sharding import PartitionSpec as P

HEADS = 14
HEAD_DIM = 128
MAXP = 3


NEG = -1e30


NT = (((1,), (1,)), ((), ()))
TN = (((0,), (0,)), ((), ()))


def shifted(value, axis, by):
    peers = lax.axis_size(axis)
    pairs = [(i, i + by) for i in range(peers) if 0 <= i + by < peers]
    return lax.ppermute(value, axis, pairs)


def segments(offsets, positions, slab_len):
    found = jnp.sum((offsets[None, :] <= positions[:, None]).astype(jnp.int32), axis=1) - 1
    inside = (positions >= 0) & (positions < slab_len)
    return jnp.where(inside, found, -1)


def allowed_of(row_seg_ref, col_seg_ref):
    width = row_seg_ref.shape[1]
    cols = jnp.transpose(jnp.broadcast_to(col_seg_ref[...], (width, width)))
    return cols == row_seg_ref[...]


def fetch(rows_hbm, kv_hbm, rows_ref, kv_ref, sems):
    copies = []
    for h in range(HEADS):
        cols = pl.ds(h * HEAD_DIM, HEAD_DIM)
        pair = (
            pltpu.make_async_copy(
                rows_hbm.at[:, :, cols], rows_ref.at[:, :, cols], sems.at[0, h]
            ),
            pltpu.make_async_copy(kv_hbm.at[:, :, cols], kv_ref.at[:, :, cols], sems.at[1, h]),
        )
        for copy in pair:
            copy.start()
        copies.append(pair)
    return copies


def arrived(copies, h):
    for copy in copies[h]:
        copy.wait()


def stats_kernel(
    flag_ref, rows_hbm, kv_hbm, row_seg_ref, col_seg_ref, out_ref, rows_ref, kv_ref, sems
):
    @pl.when(flag_ref[0] == 0)
    def _():
        out_ref[0] = jnp.full(out_ref.shape[1:], NEG, jnp.float32)
        out_ref[1] = jnp.zeros(out_ref.shape[1:], jnp.float32)
        out_ref[2] = jnp.zeros(out_ref.shape[1:], jnp.float32)

    @pl.when(flag_ref[0] != 0)
    def _():
        copies = fetch(rows_hbm, kv_hbm, rows_ref, kv_ref, sems)
        allowed = allowed_of(row_seg_ref, col_seg_ref)
        scale = HEAD_DIM ** (-0.5)
        for h in range(HEADS):
            arrived(copies, h)
            cols = slice(h * HEAD_DIM, (h + 1) * HEAD_DIM)
            query = rows_ref[0, :, cols]
            grad = rows_ref[1, :, cols]
            scores = lax.dot_general(
                kv_ref[0, :, cols], query, NT, preferred_element_type=jnp.float32
            ) * scale
            scores = jnp.where(allowed, scores, NEG)
            maximum = jnp.max(scores, axis=0, keepdims=True)
            probs = jnp.where(allowed, jnp.exp(scores - maximum), 0.0)
            dprobs = lax.dot_general(
                kv_ref[1, :, cols], grad, NT, preferred_element_type=jnp.float32
            )
            out_ref[0, h : h + 1, :] = maximum
            out_ref[1, h : h + 1, :] = jnp.sum(probs, axis=0, keepdims=True)
            out_ref[2, h : h + 1, :] = jnp.sum(probs * dprobs, axis=0, keepdims=True)


def grad_kernel(
    flag_ref, rows_hbm, final_ref, kv_hbm, row_seg_ref, col_seg_ref, gq_ref, gkv_ref,
    rows_ref, kv_ref, sems,
):

    @pl.when(flag_ref[0] == 0)
    def _():
        gq_ref[...] = jnp.zeros(gq_ref.shape, gq_ref.dtype)
        gkv_ref[...] = jnp.zeros(gkv_ref.shape, gkv_ref.dtype)

    @pl.when(flag_ref[0] != 0)
    def _():
        copies = fetch(rows_hbm, kv_hbm, rows_ref, kv_ref, sems)
        allowed = allowed_of(row_seg_ref, col_seg_ref)
        scale = HEAD_DIM ** (-0.5)
        for h in range(HEADS):
            arrived(copies, h)
            cols = slice(h * HEAD_DIM, (h + 1) * HEAD_DIM)
            query = rows_ref[0, :, cols]
            grad = rows_ref[1, :, cols]
            key = kv_ref[0, :, cols]
            log_total = final_ref[0, h : h + 1, :]
            delta = final_ref[1, h : h + 1, :]
            scores = lax.dot_general(key, query, NT, preferred_element_type=jnp.float32) * scale
            probs = jnp.where(allowed, jnp.exp(scores - log_total), 0.0)
            dprobs = lax.dot_general(
                kv_ref[1, :, cols], grad, NT, preferred_element_type=jnp.float32
            )
            dscores = jnp.where(allowed, probs * (dprobs - delta), 0.0)
            probs_low = probs.astype(jnp.bfloat16)
            dscores_low = dscores.astype(jnp.bfloat16)
            gk = jnp.dot(dscores_low, query, preferred_element_type=jnp.float32) * scale
            gv = jnp.dot(probs_low, grad, preferred_element_type=jnp.float32)
            gq = lax.dot_general(dscores_low, key, TN, preferred_element_type=jnp.float32) * scale
            gq_ref[:, cols] = gq.astype(gq_ref.dtype)
            gkv_ref[0, :, cols] = gk.astype(gkv_ref.dtype)
            gkv_ref[1, :, cols] = gv.astype(gkv_ref.dtype)


def memory_specs(*spaces):
    return [pl.BlockSpec(memory_space=space) for space in spaces]


def scratch_for(rows, kv):
    return [
        pltpu.VMEM(rows.shape, rows.dtype),
        pltpu.VMEM(kv.shape, kv.dtype),
        pltpu.SemaphoreType.DMA((2, HEADS)),
    ]


def pair_statistics(flag, rows, kv, row_segments, col_segments):
    vmem, anywhere = pltpu.VMEM, pl.ANY
    return pl.pallas_call(
        stats_kernel,
        out_shape=jax.ShapeDtypeStruct((3, HEADS, rows.shape[1]), jnp.float32),
        in_specs=memory_specs(pltpu.SMEM, anywhere, anywhere, vmem, vmem),
        scratch_shapes=scratch_for(rows, kv),
    )(flag, rows, kv, row_segments[None, :], col_segments[None, :])


def pair_gradients(flag, rows, final, kv, row_segments, col_segments, out_dtype):
    vmem, anywhere = pltpu.VMEM, pl.ANY
    return pl.pallas_call(
        grad_kernel,
        out_shape=(
            jax.ShapeDtypeStruct(rows.shape[1:], out_dtype),
            jax.ShapeDtypeStruct(kv.shape, out_dtype),
        ),
        in_specs=memory_specs(pltpu.SMEM, anywhere, vmem, anywhere, vmem, vmem),
        scratch_shapes=scratch_for(rows, kv),
    )(flag, rows, final, kv, row_segments[None, :], col_segments[None, :])


def merge_statistics(first, second):
    maximum = jnp.maximum(first[0], second[0])
    scale_one = jnp.exp(first[0] - maximum)
    scale_two = jnp.exp(second[0] - maximum)
    return (
        maximum,
        first[1] * scale_one + second[1] * scale_two,
        first[2] * scale_one + second[2] * scale_two,
    )


def finalize(statistics):
    return (statistics[0] + jnp.log(statistics[1]), statistics[2] / statistics[1])


def on_device(queries, keys, values, grad_out, offsets):
    axis = ("grp", "ctx")
    block_len = queries.shape[0]
    device_count = lax.axis_size(axis)
    slab_len = device_count * block_len
    device_index = lax.axis_index(axis)
    own_positions = device_index * block_len + jnp.arange(block_len, dtype=jnp.int32)
    own_segments = segments(offsets, own_positions, slab_len)
    rows = jnp.stack([queries, grad_out])
    kv = jnp.stack([keys, values])
    distances = [d for d in range(1, MAXP + 1)] + [-d for d in range(1, MAXP + 1)]
    always = jnp.ones((1,), jnp.int32)

    halo = {}
    up, down = kv, kv
    for distance in range(1, MAXP + 1):
        up = shifted(up, axis, -1)
        down = shifted(down, axis, 1)
        halo[distance], halo[-distance] = up, down
    received = {}
    for distance in distances:
        far_kv = halo[distance]
        far_segments = segments(offsets, own_positions + distance * block_len, slab_len)
        shared = jnp.any(far_segments[:, None] == own_segments[None, :])
        received[distance] = (far_kv, far_segments, shared)

    own = pair_statistics(always, rows, kv, own_segments, own_segments)
    row_stats = (own[0], own[1], own[2])
    for distance in distances:
        far_kv, far_segments, shared = received[distance]
        flag = shared.astype(jnp.int32).reshape(1)
        partial = pair_statistics(flag, rows, far_kv, own_segments, far_segments)
        row_stats = merge_statistics(row_stats, (partial[0], partial[1], partial[2]))
    log_total, delta_rows = finalize(row_stats)
    final_stats = jnp.stack([log_total, delta_rows])

    grad_query, grad_kv = pair_gradients(
        always, rows, final_stats, kv, own_segments, own_segments, jnp.float32
    )
    terms = {}
    for distance in sorted(distances, key=lambda d: (-abs(d), -d)):
        far_kv, far_segments, shared = received[distance]
        flag = shared.astype(jnp.int32).reshape(1)
        far_gq, terms[distance] = pair_gradients(
            flag, rows, final_stats, far_kv, own_segments, far_segments, jnp.bfloat16
        )
        grad_query = grad_query + far_gq.astype(jnp.float32)
    for sign in (1, -1):
        carried = shifted(terms[sign * MAXP], axis, sign)
        for distance in range(MAXP - 1, 0, -1):
            partial = carried.astype(jnp.float32) + terms[sign * distance].astype(jnp.float32)
            carried = shifted(partial.astype(jnp.bfloat16), axis, sign)
        grad_kv = grad_kv + carried.astype(jnp.float32)
    return (
        grad_query.astype(jnp.bfloat16),
        grad_kv[0].astype(jnp.bfloat16),
        grad_kv[1].astype(jnp.bfloat16),
    )


def solution(mesh):
    placed = (
        P(("grp", "ctx"), None),
        P(("grp", "ctx"), None),
        P(("grp", "ctx"), None),
        P(("grp", "ctx"), None),
        P(),
    )
    return jax.shard_map(
        on_device,
        mesh=mesh,
        in_specs=placed,
        out_specs=(P(("grp", "ctx"), None), P(("grp", "ctx"), None), P(("grp", "ctx"), None)),
        check_vma=False,
    )
```

```python
import functools

import jax
import jax.numpy as jnp
from jax import lax
from jax.experimental import pallas as pl
from jax.experimental.pallas import tpu as pltpu
from jax.sharding import PartitionSpec as P

HEADS = 14
HEAD_DIM = 128
MAXP = 3


NEG = -1e30


NT = (((1,), (1,)), ((), ()))
TN = (((0,), (0,)), ((), ()))


def shifted(value, axis, by):
    peers = lax.axis_size(axis)
    pairs = [(i, i + by) for i in range(peers) if 0 <= i + by < peers]
    return lax.ppermute(value, axis, pairs)


def segments(offsets, positions, slab_len):
    found = jnp.sum((offsets[None, :] <= positions[:, None]).astype(jnp.int32), axis=1) - 1
    inside = (positions >= 0) & (positions < slab_len)
    return jnp.where(inside, found, -1)


def allowed_of(row_seg_ref, col_seg_ref):
    width = row_seg_ref.shape[1]
    cols = jnp.transpose(jnp.broadcast_to(col_seg_ref[...], (width, width)))
    return cols == row_seg_ref[...]


def stats_kernel(flag_ref, rows_ref, kv_ref, row_seg_ref, col_seg_ref, out_ref):
    @pl.when(flag_ref[0] == 0)
    def _():
        out_ref[0] = jnp.full(out_ref.shape[1:], NEG, jnp.float32)
        out_ref[1] = jnp.zeros(out_ref.shape[1:], jnp.float32)
        out_ref[2] = jnp.zeros(out_ref.shape[1:], jnp.float32)

    @pl.when(flag_ref[0] != 0)
    def _():
        allowed = allowed_of(row_seg_ref, col_seg_ref)
        scale = HEAD_DIM ** (-0.5)
        for h in range(HEADS):
            cols = slice(h * HEAD_DIM, (h + 1) * HEAD_DIM)
            query = rows_ref[0, :, cols]
            grad = rows_ref[1, :, cols]
            scores = lax.dot_general(
                kv_ref[0, :, cols], query, NT, preferred_element_type=jnp.float32
            ) * scale
            scores = jnp.where(allowed, scores, NEG)
            maximum = jnp.max(scores, axis=0, keepdims=True)
            probs = jnp.where(allowed, jnp.exp(scores - maximum), 0.0)
            dprobs = lax.dot_general(
                kv_ref[1, :, cols], grad, NT, preferred_element_type=jnp.float32
            )
            out_ref[0, h : h + 1, :] = maximum
            out_ref[1, h : h + 1, :] = jnp.sum(probs, axis=0, keepdims=True)
            out_ref[2, h : h + 1, :] = jnp.sum(probs * dprobs, axis=0, keepdims=True)


def grad_kernel(flag_ref, rows_ref, final_ref, kv_ref, row_seg_ref, col_seg_ref, *refs):
    if len(refs) == 3:
        carried_ref, gq_ref, gkv_ref = refs
    else:
        carried_ref = None
        gq_ref, gkv_ref = refs

    def carry(index, cols, term):
        if carried_ref is None:
            return term.astype(gkv_ref.dtype)
        total = carried_ref[index, :, cols].astype(jnp.float32)
        if term is not None:
            total = total + term.astype(jnp.bfloat16).astype(jnp.float32)
        return total.astype(gkv_ref.dtype)

    @pl.when(flag_ref[0] == 0)
    def _():
        gq_ref[...] = jnp.zeros(gq_ref.shape, gq_ref.dtype)
        if carried_ref is None:
            gkv_ref[...] = jnp.zeros(gkv_ref.shape, gkv_ref.dtype)
        else:
            gkv_ref[...] = carried_ref[...]

    @pl.when(flag_ref[0] != 0)
    def _():
        allowed = allowed_of(row_seg_ref, col_seg_ref)
        scale = HEAD_DIM ** (-0.5)
        for h in range(HEADS):
            cols = slice(h * HEAD_DIM, (h + 1) * HEAD_DIM)
            query = rows_ref[0, :, cols]
            grad = rows_ref[1, :, cols]
            key = kv_ref[0, :, cols]
            log_total = final_ref[0, h : h + 1, :]
            delta = final_ref[1, h : h + 1, :]
            scores = lax.dot_general(key, query, NT, preferred_element_type=jnp.float32) * scale
            probs = jnp.where(allowed, jnp.exp(scores - log_total), 0.0)
            dprobs = lax.dot_general(
                kv_ref[1, :, cols], grad, NT, preferred_element_type=jnp.float32
            )
            dscores = jnp.where(allowed, probs * (dprobs - delta), 0.0)
            probs_low = probs.astype(jnp.bfloat16)
            dscores_low = dscores.astype(jnp.bfloat16)
            gk = jnp.dot(dscores_low, query, preferred_element_type=jnp.float32) * scale
            gv = jnp.dot(probs_low, grad, preferred_element_type=jnp.float32)
            gq = lax.dot_general(dscores_low, key, TN, preferred_element_type=jnp.float32) * scale
            gq_ref[:, cols] = gq.astype(gq_ref.dtype)
            gkv_ref[0, :, cols] = carry(0, cols, gk)
            gkv_ref[1, :, cols] = carry(1, cols, gv)


def vmem_specs(count):
    return [pl.BlockSpec(memory_space=pltpu.SMEM)] + [
        pl.BlockSpec(memory_space=pltpu.VMEM) for _ in range(count)
    ]


def pair_statistics(flag, rows, kv, row_segments, col_segments):
    return pl.pallas_call(
        stats_kernel,
        out_shape=jax.ShapeDtypeStruct((3, HEADS, rows.shape[1]), jnp.float32),
        in_specs=vmem_specs(4),
    )(flag, rows, kv, row_segments[None, :], col_segments[None, :])


def pair_gradients(flag, rows, final, kv, row_segments, col_segments, out_dtype, carried=None):
    operands = [flag, rows, final, kv, row_segments[None, :], col_segments[None, :]]
    if carried is not None:
        operands.append(carried)
    return pl.pallas_call(
        grad_kernel,
        out_shape=(
            jax.ShapeDtypeStruct(rows.shape[1:], out_dtype),
            jax.ShapeDtypeStruct(kv.shape, out_dtype),
        ),
        in_specs=vmem_specs(len(operands) - 1),
    )(*operands)


def merge_statistics(first, second):
    maximum = jnp.maximum(first[0], second[0])
    scale_one = jnp.exp(first[0] - maximum)
    scale_two = jnp.exp(second[0] - maximum)
    return (
        maximum,
        first[1] * scale_one + second[1] * scale_two,
        first[2] * scale_one + second[2] * scale_two,
    )


def finalize(statistics):
    return (statistics[0] + jnp.log(statistics[1]), statistics[2] / statistics[1])


def on_device(queries, keys, values, grad_out, offsets):
    axis = ("grp", "ctx")
    block_len = queries.shape[0]
    device_count = lax.axis_size(axis)
    slab_len = device_count * block_len
    device_index = lax.axis_index(axis)
    own_positions = device_index * block_len + jnp.arange(block_len, dtype=jnp.int32)
    own_segments = segments(offsets, own_positions, slab_len)
    rows = jnp.stack([queries, grad_out])
    kv = jnp.stack([keys, values])
    distances = [d for d in range(1, MAXP + 1)] + [-d for d in range(1, MAXP + 1)]
    always = jnp.ones((1,), jnp.int32)

    halo = {}
    up, down = kv, kv
    for distance in range(1, MAXP + 1):
        up = shifted(up, axis, -1)
        down = shifted(down, axis, 1)
        halo[distance], halo[-distance] = up, down
    received = {}
    for distance in distances:
        far_kv = halo[distance]
        far_segments = segments(offsets, own_positions + distance * block_len, slab_len)
        shared = jnp.any(far_segments[:, None] == own_segments[None, :])
        received[distance] = (far_kv, far_segments, shared)

    own = pair_statistics(always, rows, kv, own_segments, own_segments)
    row_stats = (own[0], own[1], own[2])
    for distance in distances:
        far_kv, far_segments, shared = received[distance]
        flag = shared.astype(jnp.int32).reshape(1)
        partial = pair_statistics(flag, rows, far_kv, own_segments, far_segments)
        row_stats = merge_statistics(row_stats, (partial[0], partial[1], partial[2]))
    log_total, delta_rows = finalize(row_stats)
    final_stats = jnp.stack([log_total, delta_rows])

    grad_query, grad_kv = pair_gradients(
        always, rows, final_stats, kv, own_segments, own_segments, jnp.float32
    )
    def term_of(distance, carried=None):
        far_kv, far_segments, shared = received[distance]
        flag = shared.astype(jnp.int32).reshape(1)
        return pair_gradients(
            flag, rows, final_stats, far_kv, own_segments, far_segments, jnp.bfloat16, carried
        )

    carried = {}
    for sign in (1, -1):
        far_gq, term = term_of(sign * MAXP)
        grad_query = grad_query + far_gq.astype(jnp.float32)
        carried[sign] = shifted(term, axis, sign)
    for distance in range(MAXP - 1, 0, -1):
        for sign in (1, -1):
            far_gq, term = term_of(sign * distance, carried[sign])
            grad_query = grad_query + far_gq.astype(jnp.float32)
            carried[sign] = shifted(term, axis, sign)
    grad_kv = grad_kv + carried[1].astype(jnp.float32) + carried[-1].astype(jnp.float32)
    return (
        grad_query.astype(jnp.bfloat16),
        grad_kv[0].astype(jnp.bfloat16),
        grad_kv[1].astype(jnp.bfloat16),
    )


def solution(mesh):
    placed = (
        P(("grp", "ctx"), None),
        P(("grp", "ctx"), None),
        P(("grp", "ctx"), None),
        P(("grp", "ctx"), None),
        P(),
    )
    return jax.shard_map(
        on_device,
        mesh=mesh,
        in_specs=placed,
        out_specs=(P(("grp", "ctx"), None), P(("grp", "ctx"), None), P(("grp", "ctx"), None)),
        check_vma=False,
    )
```

```python
import functools

import jax
import jax.numpy as jnp
from jax import lax
from jax.experimental import pallas as pl
from jax.experimental.pallas import tpu as pltpu
from jax.sharding import PartitionSpec as P

HEADS = 14
HEAD_DIM = 128
MAXP = 3


NEG = -1e30


NT = (((1,), (1,)), ((), ()))
TN = (((0,), (0,)), ((), ()))


def shifted(value, axis, by):
    peers = lax.axis_size(axis)
    pairs = [(i, i + by) for i in range(peers) if 0 <= i + by < peers]
    return lax.ppermute(value, axis, pairs)


def segments(offsets, positions, slab_len):
    found = jnp.sum((offsets[None, :] <= positions[:, None]).astype(jnp.int32), axis=1) - 1
    inside = (positions >= 0) & (positions < slab_len)
    return jnp.where(inside, found, -1)


def allowed_of(row_seg_ref, col_seg_ref):
    width = row_seg_ref.shape[1]
    cols = jnp.transpose(jnp.broadcast_to(col_seg_ref[...], (width, width)))
    return cols == row_seg_ref[...]


def stats_kernel(flag_ref, rows_ref, kv_ref, row_seg_ref, col_seg_ref, out_ref):
    @pl.when(flag_ref[0] == 0)
    def _():
        out_ref[0] = jnp.full(out_ref.shape[1:], NEG, jnp.float32)
        out_ref[1] = jnp.zeros(out_ref.shape[1:], jnp.float32)
        out_ref[2] = jnp.zeros(out_ref.shape[1:], jnp.float32)

    @pl.when(flag_ref[0] != 0)
    def _():
        allowed = allowed_of(row_seg_ref, col_seg_ref)
        scale = HEAD_DIM ** (-0.5)
        for h in range(HEADS):
            cols = slice(h * HEAD_DIM, (h + 1) * HEAD_DIM)
            query = rows_ref[0, :, cols]
            grad = rows_ref[1, :, cols]
            scores = lax.dot_general(
                kv_ref[0, :, cols], query, NT, preferred_element_type=jnp.float32
            ) * scale
            scores = jnp.where(allowed, scores, NEG)
            maximum = jnp.max(scores, axis=0, keepdims=True)
            probs = jnp.where(allowed, jnp.exp(scores - maximum), 0.0)
            dprobs = lax.dot_general(
                kv_ref[1, :, cols], grad, NT, preferred_element_type=jnp.float32
            )
            out_ref[0, h : h + 1, :] = maximum
            out_ref[1, h : h + 1, :] = jnp.sum(probs, axis=0, keepdims=True)
            out_ref[2, h : h + 1, :] = jnp.sum(probs * dprobs, axis=0, keepdims=True)


def all_stats_kernel(flags_ref, rows_ref, *refs):
    count = len(refs) - 4
    kv_refs = refs[:count]
    row_seg_ref, col_segs_ref, final_ref, stats_ref = refs[count:]
    scale = HEAD_DIM ** (-0.5)
    for pair in range(count):
        kv_ref = kv_refs[pair]

        @pl.when(flags_ref[pair] != 0)
        def _():
            cols_seg = col_segs_ref[pair : pair + 1, :]
            width = row_seg_ref.shape[1]
            allowed = jnp.transpose(jnp.broadcast_to(cols_seg, (width, width))) == row_seg_ref[...]
            for h in range(HEADS):
                cols = slice(h * HEAD_DIM, (h + 1) * HEAD_DIM)
                query = rows_ref[0, :, cols]
                grad = rows_ref[1, :, cols]
                scores = lax.dot_general(
                    kv_ref[0, :, cols], query, NT, preferred_element_type=jnp.float32
                ) * scale
                scores = jnp.where(allowed, scores, NEG)
                maximum = jnp.max(scores, axis=0, keepdims=True)
                probs = jnp.where(allowed, jnp.exp(scores - maximum), 0.0)
                dprobs = lax.dot_general(
                    kv_ref[1, :, cols], grad, NT, preferred_element_type=jnp.float32
                )
                total = jnp.sum(probs, axis=0, keepdims=True)
                dot = jnp.sum(probs * dprobs, axis=0, keepdims=True)
                if pair == 0:
                    stats_ref[0, h : h + 1, :] = maximum
                    stats_ref[1, h : h + 1, :] = total
                    stats_ref[2, h : h + 1, :] = dot
                else:
                    first = (
                        stats_ref[0, h : h + 1, :],
                        stats_ref[1, h : h + 1, :],
                        stats_ref[2, h : h + 1, :],
                    )
                    merged = merge_statistics(first, (maximum, total, dot))
                    for index in range(3):
                        stats_ref[index, h : h + 1, :] = merged[index]

    log_total, delta = finalize((stats_ref[0], stats_ref[1], stats_ref[2]))
    final_ref[0] = log_total
    final_ref[1] = delta


def final_statistics(flags, rows, kvs, row_segments, col_segments):
    return pl.pallas_call(
        all_stats_kernel,
        out_shape=jax.ShapeDtypeStruct((2, HEADS, rows.shape[1]), jnp.float32),
        in_specs=vmem_specs(len(kvs) + 3),
        scratch_shapes=[pltpu.VMEM((3, HEADS, rows.shape[1]), jnp.float32)],
    )(flags, rows, *kvs, row_segments[None, :], col_segments)


def grad_kernel(flag_ref, rows_ref, final_ref, kv_ref, row_seg_ref, col_seg_ref, gq_ref, gkv_ref):

    @pl.when(flag_ref[0] == 0)
    def _():
        gq_ref[...] = jnp.zeros(gq_ref.shape, gq_ref.dtype)
        gkv_ref[...] = jnp.zeros(gkv_ref.shape, gkv_ref.dtype)

    @pl.when(flag_ref[0] != 0)
    def _():
        allowed = allowed_of(row_seg_ref, col_seg_ref)
        scale = HEAD_DIM ** (-0.5)
        for h in range(HEADS):
            cols = slice(h * HEAD_DIM, (h + 1) * HEAD_DIM)
            query = rows_ref[0, :, cols]
            grad = rows_ref[1, :, cols]
            key = kv_ref[0, :, cols]
            log_total = final_ref[0, h : h + 1, :]
            delta = final_ref[1, h : h + 1, :]
            scores = lax.dot_general(key, query, NT, preferred_element_type=jnp.float32) * scale
            probs = jnp.where(allowed, jnp.exp(scores - log_total), 0.0)
            dprobs = lax.dot_general(
                kv_ref[1, :, cols], grad, NT, preferred_element_type=jnp.float32
            )
            dscores = jnp.where(allowed, probs * (dprobs - delta), 0.0)
            probs_low = probs.astype(jnp.bfloat16)
            dscores_low = dscores.astype(jnp.bfloat16)
            gk = jnp.dot(dscores_low, query, preferred_element_type=jnp.float32) * scale
            gv = jnp.dot(probs_low, grad, preferred_element_type=jnp.float32)
            gq = lax.dot_general(dscores_low, key, TN, preferred_element_type=jnp.float32) * scale
            gq_ref[:, cols] = gq.astype(gq_ref.dtype)
            gkv_ref[0, :, cols] = gk.astype(gkv_ref.dtype)
            gkv_ref[1, :, cols] = gv.astype(gkv_ref.dtype)


def vmem_specs(count):
    return [pl.BlockSpec(memory_space=pltpu.SMEM)] + [
        pl.BlockSpec(memory_space=pltpu.VMEM) for _ in range(count)
    ]


def pair_statistics(flag, rows, kv, row_segments, col_segments):
    return pl.pallas_call(
        stats_kernel,
        out_shape=jax.ShapeDtypeStruct((3, HEADS, rows.shape[1]), jnp.float32),
        in_specs=vmem_specs(4),
    )(flag, rows, kv, row_segments[None, :], col_segments[None, :])


def pair_gradients(flag, rows, final, kv, row_segments, col_segments, out_dtype):
    return pl.pallas_call(
        grad_kernel,
        out_shape=(
            jax.ShapeDtypeStruct(rows.shape[1:], out_dtype),
            jax.ShapeDtypeStruct(kv.shape, out_dtype),
        ),
        in_specs=vmem_specs(5),
    )(flag, rows, final, kv, row_segments[None, :], col_segments[None, :])


def merge_statistics(first, second):
    maximum = jnp.maximum(first[0], second[0])
    scale_one = jnp.exp(first[0] - maximum)
    scale_two = jnp.exp(second[0] - maximum)
    return (
        maximum,
        first[1] * scale_one + second[1] * scale_two,
        first[2] * scale_one + second[2] * scale_two,
    )


def finalize(statistics):
    return (statistics[0] + jnp.log(statistics[1]), statistics[2] / statistics[1])


def on_device(queries, keys, values, grad_out, offsets):
    axis = ("grp", "ctx")
    block_len = queries.shape[0]
    device_count = lax.axis_size(axis)
    slab_len = device_count * block_len
    device_index = lax.axis_index(axis)
    own_positions = device_index * block_len + jnp.arange(block_len, dtype=jnp.int32)
    own_segments = segments(offsets, own_positions, slab_len)
    rows = jnp.stack([queries, grad_out])
    kv = jnp.stack([keys, values])
    distances = [d for d in range(1, MAXP + 1)] + [-d for d in range(1, MAXP + 1)]
    always = jnp.ones((1,), jnp.int32)

    halo = {}
    up, down = kv, kv
    for distance in range(1, MAXP + 1):
        up = shifted(up, axis, -1)
        down = shifted(down, axis, 1)
        halo[distance], halo[-distance] = up, down
    received = {}
    for distance in distances:
        far_kv = halo[distance]
        far_segments = segments(offsets, own_positions + distance * block_len, slab_len)
        shared = jnp.any(far_segments[:, None] == own_segments[None, :])
        received[distance] = (far_kv, far_segments, shared)

    flags = jnp.stack([jnp.ones((), jnp.int32)] + [
        received[distance][2].astype(jnp.int32) for distance in distances
    ])
    col_segments = jnp.stack([own_segments] + [received[distance][1] for distance in distances])
    final_stats = final_statistics(
        flags, rows, [kv] + [received[distance][0] for distance in distances],
        own_segments, col_segments,
    )

    grad_query, grad_kv = pair_gradients(
        always, rows, final_stats, kv, own_segments, own_segments, jnp.float32
    )
    terms = {}
    for distance in sorted(distances, key=lambda d: (-abs(d), -d)):
        far_kv, far_segments, shared = received[distance]
        flag = shared.astype(jnp.int32).reshape(1)
        far_gq, terms[distance] = pair_gradients(
            flag, rows, final_stats, far_kv, own_segments, far_segments, jnp.bfloat16
        )
        grad_query = grad_query + far_gq.astype(jnp.float32)
    for sign in (1, -1):
        carried = shifted(terms[sign * MAXP], axis, sign)
        for distance in range(MAXP - 1, 0, -1):
            partial = carried.astype(jnp.float32) + terms[sign * distance].astype(jnp.float32)
            carried = shifted(partial.astype(jnp.bfloat16), axis, sign)
        grad_kv = grad_kv + carried.astype(jnp.float32)
    return (
        grad_query.astype(jnp.bfloat16),
        grad_kv[0].astype(jnp.bfloat16),
        grad_kv[1].astype(jnp.bfloat16),
    )


def solution(mesh):
    placed = (
        P(("grp", "ctx"), None),
        P(("grp", "ctx"), None),
        P(("grp", "ctx"), None),
        P(("grp", "ctx"), None),
        P(),
    )
    return jax.shard_map(
        on_device,
        mesh=mesh,
        in_specs=placed,
        out_specs=(P(("grp", "ctx"), None), P(("grp", "ctx"), None), P(("grp", "ctx"), None)),
        check_vma=False,
    )
```

```python
import functools

import jax
import jax.numpy as jnp
from jax import lax
from jax.experimental import pallas as pl
from jax.experimental.pallas import tpu as pltpu
from jax.sharding import PartitionSpec as P

HEADS = 14
HEAD_DIM = 128
MAXP = 3


NEG = -1e30


NT = (((1,), (1,)), ((), ()))
TN = (((0,), (0,)), ((), ()))


def shifted(value, axis, by):
    peers = lax.axis_size(axis)
    pairs = [(i, i + by) for i in range(peers) if 0 <= i + by < peers]
    return lax.ppermute(value, axis, pairs)


def segments(offsets, positions, slab_len):
    found = jnp.sum((offsets[None, :] <= positions[:, None]).astype(jnp.int32), axis=1) - 1
    inside = (positions >= 0) & (positions < slab_len)
    return jnp.where(inside, found, -1)


def allowed_of(row_seg_ref, col_seg_ref):
    width = row_seg_ref.shape[1]
    cols = jnp.transpose(jnp.broadcast_to(col_seg_ref[...], (width, width)))
    return cols == row_seg_ref[...]


def stats_kernel(flag_ref, query_ref, grad_ref, kv_ref, row_seg_ref, col_seg_ref, out_ref):
    @pl.when(flag_ref[0] == 0)
    def _():
        out_ref[0] = jnp.full(out_ref.shape[1:], NEG, jnp.float32)
        out_ref[1] = jnp.zeros(out_ref.shape[1:], jnp.float32)
        out_ref[2] = jnp.zeros(out_ref.shape[1:], jnp.float32)

    @pl.when(flag_ref[0] != 0)
    def _():
        allowed = allowed_of(row_seg_ref, col_seg_ref)
        scale = HEAD_DIM ** (-0.5)
        for h in range(HEADS):
            cols = slice(h * HEAD_DIM, (h + 1) * HEAD_DIM)
            query = query_ref[:, cols]
            grad = grad_ref[:, cols]
            scores = lax.dot_general(
                kv_ref[0, :, cols], query, NT, preferred_element_type=jnp.float32
            ) * scale
            scores = jnp.where(allowed, scores, NEG)
            maximum = jnp.max(scores, axis=0, keepdims=True)
            probs = jnp.where(allowed, jnp.exp(scores - maximum), 0.0)
            dprobs = lax.dot_general(
                kv_ref[1, :, cols], grad, NT, preferred_element_type=jnp.float32
            )
            out_ref[0, h : h + 1, :] = maximum
            out_ref[1, h : h + 1, :] = jnp.sum(probs, axis=0, keepdims=True)
            out_ref[2, h : h + 1, :] = jnp.sum(probs * dprobs, axis=0, keepdims=True)


def grad_kernel(flag_ref, query_ref, grad_ref, final_ref, kv_ref, row_seg_ref, col_seg_ref, gq_ref, gkv_ref):

    @pl.when(flag_ref[0] == 0)
    def _():
        gq_ref[...] = jnp.zeros(gq_ref.shape, gq_ref.dtype)
        gkv_ref[...] = jnp.zeros(gkv_ref.shape, gkv_ref.dtype)

    @pl.when(flag_ref[0] != 0)
    def _():
        allowed = allowed_of(row_seg_ref, col_seg_ref)
        scale = HEAD_DIM ** (-0.5)
        for h in range(HEADS):
            cols = slice(h * HEAD_DIM, (h + 1) * HEAD_DIM)
            query = query_ref[:, cols]
            grad = grad_ref[:, cols]
            key = kv_ref[0, :, cols]
            log_total = final_ref[0, h : h + 1, :]
            delta = final_ref[1, h : h + 1, :]
            scores = lax.dot_general(key, query, NT, preferred_element_type=jnp.float32) * scale
            probs = jnp.where(allowed, jnp.exp(scores - log_total), 0.0)
            dprobs = lax.dot_general(
                kv_ref[1, :, cols], grad, NT, preferred_element_type=jnp.float32
            )
            dscores = jnp.where(allowed, probs * (dprobs - delta), 0.0)
            probs_low = probs.astype(jnp.bfloat16)
            dscores_low = dscores.astype(jnp.bfloat16)
            gk = jnp.dot(dscores_low, query, preferred_element_type=jnp.float32) * scale
            gv = jnp.dot(probs_low, grad, preferred_element_type=jnp.float32)
            gq = lax.dot_general(dscores_low, key, TN, preferred_element_type=jnp.float32) * scale
            gq_ref[:, cols] = gq.astype(gq_ref.dtype)
            gkv_ref[0, :, cols] = gk.astype(gkv_ref.dtype)
            gkv_ref[1, :, cols] = gv.astype(gkv_ref.dtype)


def vmem_specs(count):
    return [pl.BlockSpec(memory_space=pltpu.SMEM)] + [
        pl.BlockSpec(memory_space=pltpu.VMEM) for _ in range(count)
    ]


def pair_statistics(flag, rows, kv, row_segments, col_segments):
    return pl.pallas_call(
        stats_kernel,
        out_shape=jax.ShapeDtypeStruct((3, HEADS, rows[0].shape[0]), jnp.float32),
        in_specs=vmem_specs(5),
    )(flag, rows[0], rows[1], kv, row_segments[None, :], col_segments[None, :])


def pair_gradients(flag, rows, final, kv, row_segments, col_segments, out_dtype):
    return pl.pallas_call(
        grad_kernel,
        out_shape=(
            jax.ShapeDtypeStruct(rows[0].shape, out_dtype),
            jax.ShapeDtypeStruct(kv.shape, out_dtype),
        ),
        in_specs=vmem_specs(6),
    )(flag, rows[0], rows[1], final, kv, row_segments[None, :], col_segments[None, :])


def merge_statistics(first, second):
    maximum = jnp.maximum(first[0], second[0])
    scale_one = jnp.exp(first[0] - maximum)
    scale_two = jnp.exp(second[0] - maximum)
    return (
        maximum,
        first[1] * scale_one + second[1] * scale_two,
        first[2] * scale_one + second[2] * scale_two,
    )


def finalize(statistics):
    return (statistics[0] + jnp.log(statistics[1]), statistics[2] / statistics[1])


def on_device(queries, keys, values, grad_out, offsets):
    axis = ("grp", "ctx")
    block_len = queries.shape[0]
    device_count = lax.axis_size(axis)
    slab_len = device_count * block_len
    device_index = lax.axis_index(axis)
    own_positions = device_index * block_len + jnp.arange(block_len, dtype=jnp.int32)
    own_segments = segments(offsets, own_positions, slab_len)
    rows = (queries, grad_out)
    kv = jnp.stack([keys, values])
    distances = [d for d in range(1, MAXP + 1)] + [-d for d in range(1, MAXP + 1)]
    always = jnp.ones((1,), jnp.int32)

    halo = {}
    up, down = kv, kv
    for distance in range(1, MAXP + 1):
        up = shifted(up, axis, -1)
        down = shifted(down, axis, 1)
        halo[distance], halo[-distance] = up, down
    received = {}
    for distance in distances:
        far_kv = halo[distance]
        far_segments = segments(offsets, own_positions + distance * block_len, slab_len)
        shared = jnp.any(far_segments[:, None] == own_segments[None, :])
        received[distance] = (far_kv, far_segments, shared)

    own = pair_statistics(always, rows, kv, own_segments, own_segments)
    row_stats = (own[0], own[1], own[2])
    for distance in distances:
        far_kv, far_segments, shared = received[distance]
        flag = shared.astype(jnp.int32).reshape(1)
        partial = pair_statistics(flag, rows, far_kv, own_segments, far_segments)
        row_stats = merge_statistics(row_stats, (partial[0], partial[1], partial[2]))
    log_total, delta_rows = finalize(row_stats)
    final_stats = jnp.stack([log_total, delta_rows])

    grad_query, grad_kv = pair_gradients(
        always, rows, final_stats, kv, own_segments, own_segments, jnp.float32
    )
    terms = {}
    for distance in sorted(distances, key=lambda d: (-abs(d), -d)):
        far_kv, far_segments, shared = received[distance]
        flag = shared.astype(jnp.int32).reshape(1)
        far_gq, terms[distance] = pair_gradients(
            flag, rows, final_stats, far_kv, own_segments, far_segments, jnp.bfloat16
        )
        grad_query = grad_query + far_gq.astype(jnp.float32)
    for sign in (1, -1):
        carried = shifted(terms[sign * MAXP], axis, sign)
        for distance in range(MAXP - 1, 0, -1):
            partial = carried.astype(jnp.float32) + terms[sign * distance].astype(jnp.float32)
            carried = shifted(partial.astype(jnp.bfloat16), axis, sign)
        grad_kv = grad_kv + carried.astype(jnp.float32)
    return (
        grad_query.astype(jnp.bfloat16),
        grad_kv[0].astype(jnp.bfloat16),
        grad_kv[1].astype(jnp.bfloat16),
    )


def solution(mesh):
    placed = (
        P(("grp", "ctx"), None),
        P(("grp", "ctx"), None),
        P(("grp", "ctx"), None),
        P(("grp", "ctx"), None),
        P(),
    )
    return jax.shard_map(
        on_device,
        mesh=mesh,
        in_specs=placed,
        out_specs=(P(("grp", "ctx"), None), P(("grp", "ctx"), None), P(("grp", "ctx"), None)),
        check_vma=False,
    )
```

```python
import functools

import jax
import jax.numpy as jnp
from jax import lax
from jax.experimental import pallas as pl
from jax.experimental.pallas import tpu as pltpu
from jax.sharding import PartitionSpec as P

HEADS = 14
HEAD_DIM = 128
MAXP = 3


NEG = -1e30


NT = (((1,), (1,)), ((), ()))
TN = (((0,), (0,)), ((), ()))


def shifted(value, axis, by):
    peers = lax.axis_size(axis)
    pairs = [(i, i + by) for i in range(peers) if 0 <= i + by < peers]
    return lax.ppermute(value, axis, pairs)


def segments(offsets, positions, slab_len):
    found = jnp.sum((offsets[None, :] <= positions[:, None]).astype(jnp.int32), axis=1) - 1
    inside = (positions >= 0) & (positions < slab_len)
    return jnp.where(inside, found, -1)


def allowed_of(row_seg_ref, col_seg_ref):
    width = row_seg_ref.shape[1]
    cols = jnp.transpose(jnp.broadcast_to(col_seg_ref[...], (width, width)))
    return cols == row_seg_ref[...]


def stats_kernel(flag_ref, rows_ref, kv_ref, row_seg_ref, col_seg_ref, out_ref):
    @pl.when(flag_ref[0] == 0)
    def _():
        out_ref[0] = jnp.full(out_ref.shape[1:], NEG, jnp.float32)
        out_ref[1] = jnp.zeros(out_ref.shape[1:], jnp.float32)
        out_ref[2] = jnp.zeros(out_ref.shape[1:], jnp.float32)

    @pl.when(flag_ref[0] != 0)
    def _():
        allowed = allowed_of(row_seg_ref, col_seg_ref)
        scale = HEAD_DIM ** (-0.5)
        for h in range(HEADS):
            cols = slice(h * HEAD_DIM, (h + 1) * HEAD_DIM)
            query = rows_ref[0, :, cols]
            grad = rows_ref[1, :, cols]
            scores = lax.dot_general(
                kv_ref[0, :, cols], query, NT, preferred_element_type=jnp.float32
            ) * scale
            scores = jnp.where(allowed, scores, NEG)
            maximum = jnp.max(scores, axis=0, keepdims=True)
            probs = jnp.where(allowed, jnp.exp(scores - maximum), 0.0)
            dprobs = lax.dot_general(
                kv_ref[1, :, cols], grad, NT, preferred_element_type=jnp.float32
            )
            out_ref[0, h : h + 1, :] = maximum
            out_ref[1, h : h + 1, :] = jnp.sum(probs, axis=0, keepdims=True)
            out_ref[2, h : h + 1, :] = jnp.sum(probs * dprobs, axis=0, keepdims=True)


def grad_kernel(flag_ref, rows_ref, final_ref, kv_ref, row_seg_ref, col_seg_ref, gq_ref, gkv_ref):

    @pl.when(flag_ref[0] == 0)
    def _():
        gq_ref[...] = jnp.zeros(gq_ref.shape, gq_ref.dtype)
        gkv_ref[...] = jnp.zeros(gkv_ref.shape, gkv_ref.dtype)

    @pl.when(flag_ref[0] != 0)
    def _():
        allowed = allowed_of(row_seg_ref, col_seg_ref)
        scale = HEAD_DIM ** (-0.5)
        for h in range(HEADS):
            cols = slice(h * HEAD_DIM, (h + 1) * HEAD_DIM)
            query = rows_ref[0, :, cols]
            grad = rows_ref[1, :, cols]
            key = kv_ref[0, :, cols]
            log_total = final_ref[0, h : h + 1, :]
            delta = final_ref[1, h : h + 1, :]
            scores = lax.dot_general(key, query, NT, preferred_element_type=jnp.float32) * scale
            probs = jnp.where(allowed, jnp.exp(scores - log_total), 0.0)
            dprobs = lax.dot_general(
                kv_ref[1, :, cols], grad, NT, preferred_element_type=jnp.float32
            )
            dscores = jnp.where(allowed, probs * (dprobs - delta), 0.0)
            probs_low = probs.astype(jnp.bfloat16)
            dscores_low = dscores.astype(jnp.bfloat16)
            gk = jnp.dot(dscores_low, query, preferred_element_type=jnp.float32) * scale
            gv = jnp.dot(probs_low, grad, preferred_element_type=jnp.float32)
            gq = lax.dot_general(dscores_low, key, TN, preferred_element_type=jnp.float32) * scale
            gq_ref[:, cols] = gq.astype(gq_ref.dtype)
            gkv_ref[0, :, cols] = gk.astype(gkv_ref.dtype)
            gkv_ref[1, :, cols] = gv.astype(gkv_ref.dtype)


def vmem_specs(count):
    return [pl.BlockSpec(memory_space=pltpu.SMEM)] + [
        pl.BlockSpec(memory_space=pltpu.VMEM) for _ in range(count)
    ]


def pair_statistics(flag, rows, kv, row_segments, col_segments):
    return pl.pallas_call(
        stats_kernel,
        out_shape=jax.ShapeDtypeStruct((3, HEADS, rows.shape[1]), jnp.float32),
        in_specs=vmem_specs(4),
    )(flag, rows, kv, row_segments[None, :], col_segments[None, :])


def pair_gradients(flag, rows, final, kv, row_segments, col_segments, out_dtype):
    return pl.pallas_call(
        grad_kernel,
        out_shape=(
            jax.ShapeDtypeStruct(rows.shape[1:], out_dtype),
            jax.ShapeDtypeStruct(kv.shape, out_dtype),
        ),
        in_specs=vmem_specs(5),
    )(flag, rows, final, kv, row_segments[None, :], col_segments[None, :])


def merge_statistics(first, second):
    maximum = jnp.maximum(first[0], second[0])
    scale_one = jnp.exp(first[0] - maximum)
    scale_two = jnp.exp(second[0] - maximum)
    return (
        maximum,
        first[1] * scale_one + second[1] * scale_two,
        first[2] * scale_one + second[2] * scale_two,
    )


def finalize(statistics):
    return (statistics[0] + jnp.log(statistics[1]), statistics[2] / statistics[1])


def on_device(queries, keys, values, grad_out, offsets):
    axis = ("grp", "ctx")
    block_len = queries.shape[0]
    device_count = lax.axis_size(axis)
    slab_len = device_count * block_len
    device_index = lax.axis_index(axis)
    own_positions = device_index * block_len + jnp.arange(block_len, dtype=jnp.int32)
    own_segments = segments(offsets, own_positions, slab_len)
    rows = jnp.stack([queries, grad_out])
    kv = jnp.stack([keys, values])
    distances = [s * d for d in range(1, MAXP + 1) for s in (1, -1)]
    always = jnp.ones((1,), jnp.int32)

    halo = {}
    up, down = kv, kv
    for distance in range(1, MAXP + 1):
        up = shifted(up, axis, -1)
        down = shifted(down, axis, 1)
        halo[distance], halo[-distance] = up, down
    received = {}
    for distance in distances:
        far_kv = halo[distance]
        far_segments = segments(offsets, own_positions + distance * block_len, slab_len)
        shared = jnp.any(far_segments[:, None] == own_segments[None, :])
        received[distance] = (far_kv, far_segments, shared)

    own = pair_statistics(always, rows, kv, own_segments, own_segments)
    row_stats = (own[0], own[1], own[2])
    for distance in distances:
        far_kv, far_segments, shared = received[distance]
        flag = shared.astype(jnp.int32).reshape(1)
        partial = pair_statistics(flag, rows, far_kv, own_segments, far_segments)
        row_stats = merge_statistics(row_stats, (partial[0], partial[1], partial[2]))
    log_total, delta_rows = finalize(row_stats)
    final_stats = jnp.stack([log_total, delta_rows])

    grad_query, grad_kv = pair_gradients(
        always, rows, final_stats, kv, own_segments, own_segments, jnp.float32
    )
    terms = {}
    for distance in sorted(distances, key=lambda d: (-abs(d), -d)):
        far_kv, far_segments, shared = received[distance]
        flag = shared.astype(jnp.int32).reshape(1)
        far_gq, terms[distance] = pair_gradients(
            flag, rows, final_stats, far_kv, own_segments, far_segments, jnp.bfloat16
        )
        grad_query = grad_query + far_gq.astype(jnp.float32)
    for sign in (1, -1):
        carried = shifted(terms[sign * MAXP], axis, sign)
        for distance in range(MAXP - 1, 0, -1):
            partial = carried.astype(jnp.float32) + terms[sign * distance].astype(jnp.float32)
            carried = shifted(partial.astype(jnp.bfloat16), axis, sign)
        grad_kv = grad_kv + carried.astype(jnp.float32)
    return (
        grad_query.astype(jnp.bfloat16),
        grad_kv[0].astype(jnp.bfloat16),
        grad_kv[1].astype(jnp.bfloat16),
    )


def solution(mesh):
    placed = (
        P(("grp", "ctx"), None),
        P(("grp", "ctx"), None),
        P(("grp", "ctx"), None),
        P(("grp", "ctx"), None),
        P(),
    )
    return jax.shard_map(
        on_device,
        mesh=mesh,
        in_specs=placed,
        out_specs=(P(("grp", "ctx"), None), P(("grp", "ctx"), None), P(("grp", "ctx"), None)),
        check_vma=False,
    )
```
